32 devices in a mesh: groups: 2 (over x), blocks: 16 (over z, y, core).
Axes of the slice: x: 2, y: 2, z: 4, core: 2. Of those that a mesh axis runs over, the one named last changes fastest.
Arguments:
- source_coords: bfloat16 [30, 32768], P(None, ('groups', 'blocks')), parts along dimension 1
- target_coords: bfloat16 [30, 32768], P(None, ('groups', 'blocks')), parts along dimension 1
- target_potential: float32 [32768], P(('groups', 'blocks')), parts along dimension 0, may hold values from -8 to 8
- fetch_blocks: int32 [32, 16, 2], P(('groups', 'blocks')), parts along dimension 0, may hold values from 0 to 127, as said below
- pair_slots: int32 [256, 32], P(('groups', 'blocks')), parts along dimension 0, may hold values from 0 to 31, as said below
- pair_counts: int32 [256], P(('groups', 'blocks')), parts along dimension 0, may hold values from 1 to 32
Outputs:
- source_potential: float32 [32768], P(('groups', 'blocks')), parts along dimension 0
- target_potential_out: float32 [32768], P(('groups', 'blocks')), parts along dimension 0
- drift: float32 [30, 32768], P(None, ('groups', 'blocks')), parts along dimension 1
The draws below stay inside these ranges and needn't reach their ends.
There are 2 independent parts, one for each index of `groups`. The reference program is written for one: setup_inputs(seed, part) draws one part's arguments, and reference() takes and returns one part's arrays. A program takes and returns all parts, laid end to end along the dimension named above; each array names one. Nothing has to cross between parts.
Inputs may be any that keep to these rules, and one draw needn't show every extreme that they name: `fetch_blocks`: entry [d, o, c] is a target block owned by device o, that is between o * 8 and o * 8 + 7; the 2 entries of one [d, o] are distinct. `pair_slots`: entry [s, p] names entry (o, c) of the fetch list of device s // 8 as o * 2 + c; the 32 entries of a row are distinct; entries at p >= pair_counts[s] are unused.
All inputs are finite; a program needn't handle non-finite values.
Results may differ from the reference program's by a relative error of at most 0.00095.
Values may be sent and summed in bfloat16 or wider, within the bound.
No kernel may reach another device: no remote copies, remote signals or barrier semaphores. Data moves between devices by JAX's collectives and lax.ppermute only.
A program may use at most 64 MiB of HBM per device.

```python
import math
import jax
import jax.numpy as jnp
from jax import lax

PC = 30
BS = 128
SB_DEV = 8
CAP = 2
MOST_KEPT_TARGETS = 32
SWEEPS = 2
CLUSTER_BLOCKS = 128
NCELLS = 16384
FETCH_SLOTS = 32


def draw_source_coords(key, part):
    base = jax.random.fold_in(key, 1)
    random_keys = jax.random.split(base, 2)
    centres = 0.5 * jax.random.normal(random_keys[0], (PC, CLUSTER_BLOCKS, 1), jnp.float32)
    spread = 0.5 * jax.random.normal(random_keys[1], (PC, CLUSTER_BLOCKS, BS), jnp.float32)
    return (centres + spread).reshape(PC, CLUSTER_BLOCKS * BS).astype(jnp.bfloat16)


def draw_target_coords(key, part):
    base = jax.random.fold_in(key, 2)
    random_keys = jax.random.split(base, 2)
    centres = 0.5 * jax.random.normal(random_keys[0], (PC, CLUSTER_BLOCKS, 1), jnp.float32)
    spread = 0.5 * jax.random.normal(random_keys[1], (PC, CLUSTER_BLOCKS, BS), jnp.float32)
    return (centres + spread).reshape(PC, CLUSTER_BLOCKS * BS).astype(jnp.bfloat16)


def shuffled(single_random_key):
    return jax.random.permutation(single_random_key, FETCH_SLOTS)


def draw_pair_slots(key, part):
    base = jax.random.fold_in(key, 3)
    device_total = CLUSTER_BLOCKS // SB_DEV
    random_keys = jax.random.split(base, device_total + 1)
    orders = jax.vmap(shuffled)(random_keys[1:]).astype(jnp.int32)
    block_offsets = jax.random.randint(random_keys[0], (CLUSTER_BLOCKS, 1), 0, FETCH_SLOTS)
    slot_position = (block_offsets + jnp.arange(MOST_KEPT_TARGETS, dtype=jnp.int32)[None, :]) % FETCH_SLOTS
    device = jnp.arange(CLUSTER_BLOCKS, dtype=jnp.int32) // SB_DEV
    return jnp.take_along_axis(orders[device], slot_position, axis=1).astype(jnp.int32)


def draw_pair_counts(key, part):
    base = jax.random.fold_in(key, 4)
    random_keys = jax.random.split(base, 3)
    counts = jax.random.randint(random_keys[0], (CLUSTER_BLOCKS,), 1, MOST_KEPT_TARGETS + 1)
    first = jax.random.randint(random_keys[1], (), 0, CLUSTER_BLOCKS)
    second = (first + 1 + jax.random.randint(random_keys[2], (), 0, CLUSTER_BLOCKS - 1)) % CLUSTER_BLOCKS
    counts = counts.at[first].set(MOST_KEPT_TARGETS).at[second].set(1)
    return counts.astype(jnp.int32)


def draw_fetch_blocks(key, part):
    base = jax.random.fold_in(key, 5)
    random_keys = jax.random.split(base, 3)
    device_total = CLUSTER_BLOCKS // SB_DEV
    start = jax.random.randint(random_keys[0], (device_total, device_total, 1), 0, SB_DEV)
    skipped = jax.random.randint(random_keys[1], (1, device_total, 1), 0, SB_DEV)
    ranking = jax.random.permutation(random_keys[2], device_total).astype(jnp.int32)
    sparse_total = min(8, max(4, device_total // 16))
    thinned = (ranking < sparse_total)[None, :, None]
    window = jnp.arange(CAP, dtype=jnp.int32)[None, None, :]
    cycled = (start % (SB_DEV - 1) + window) % (SB_DEV - 1)
    avoiding = (skipped + 1 + cycled) % SB_DEV
    drawn = (start + window) % SB_DEV
    local = jnp.where(thinned, avoiding, drawn)
    owner = jnp.arange(device_total, dtype=jnp.int32)[None, :, None]
    return (owner * SB_DEV + local).astype(jnp.int32)


def block_levels(key, shape, cuts, low, largest):
    level = 1.0
    for dim, parts in cuts:
        heights = jax.random.uniform(jax.random.fold_in(jax.random.fold_in(key, 6), dim), (parts,), jnp.float32, low / len(cuts), largest / len(cuts))
        level = level * jnp.repeat(jnp.exp(heights), shape[dim] // parts).reshape((-1,) + (1,) * (len(shape) - 1 - dim))
    return level


def bell_draw(stream_key, shape, scale, reach, pieces=(), held_as=jnp.bfloat16):
    values = scale * jax.random.normal(stream_key, shape, jnp.float32)
    if pieces:
        values = values * block_levels(stream_key, shape, pieces, -0.22, 0.18)
    return jnp.clip(values, -reach, reach).astype(held_as)


def setup_inputs(seed: int = 0, part: int = 0) -> dict:
    key_of = jax.random.split(jax.random.key(seed), 7)
    part_splits = jax.random.split(jax.random.fold_in(key_of[6], part), 7)
    source_coords = draw_source_coords(jax.random.fold_in(jax.random.fold_in(key_of[6], part), 71), part)
    target_coords = draw_target_coords(jax.random.fold_in(jax.random.fold_in(key_of[6], part), 71), part)
    target_potential = bell_draw(part_splits[2], (NCELLS,), 2.0, 8.0, ((0, 16),), jnp.float32)
    fetch_blocks = draw_fetch_blocks(jax.random.fold_in(jax.random.fold_in(key_of[6], part), 71), part)
    pair_slots = draw_pair_slots(jax.random.fold_in(jax.random.fold_in(key_of[6], part), 71), part)
    pair_counts = draw_pair_counts(jax.random.fold_in(jax.random.fold_in(key_of[6], part), 71), part)
    return dict(source_coords=source_coords, target_coords=target_coords, target_potential=target_potential, fetch_blocks=fetch_blocks, pair_slots=pair_slots, pair_counts=pair_counts)


cost_scale = 0.25
floor_value = -1.0e30


def block_layout(coords):
    return jnp.transpose(coords.astype(jnp.float32).reshape(PC, CLUSTER_BLOCKS, BS), (1, 0, 2))


def distances(source_block, source_norm, target_group, target_norm):
    products = jnp.einsum("di,pdj->pij", source_block, target_group, precision=lax.Precision.HIGHEST)
    return (source_norm[None, :, None] + target_norm[:, None, :] - 2.0 * products) * cost_scale


def reference(source_coords, target_coords, target_potential, fetch_blocks, pair_slots, pair_counts):
    log_mass = -math.log(NCELLS)
    sources = block_layout(source_coords)
    targets = block_layout(target_coords)
    source_norms = jnp.sum(sources * sources, axis=1)
    target_norms = jnp.sum(targets * targets, axis=1)
    device_rows = (jnp.arange(CLUSTER_BLOCKS, dtype=jnp.int32) // SB_DEV)[:, None]
    partners = fetch_blocks[device_rows, pair_slots // CAP, pair_slots % CAP]
    allowed = jnp.arange(MOST_KEPT_TARGETS, dtype=jnp.int32)[None, :] < pair_counts[:, None]
    block_ids = jnp.arange(CLUSTER_BLOCKS, dtype=jnp.int32)

    def block_scores(index, potential):
        chosen = partners[index]
        return chosen, potential[chosen][:, None, :] - distances(sources[index], source_norms[index], targets[chosen], target_norms[chosen])

    def row_pass(potential):
        def one_block(index):
            chosen, scores = block_scores(index, potential)
            mask = allowed[index][:, None, None]
            maxima = jnp.max(jnp.where(mask, scores, floor_value), axis=(0, 2))
            totals = jnp.sum(jnp.where(mask, jnp.exp(scores - maxima[None, :, None]), 0.0), axis=(0, 2))
            return maxima, totals
        return lax.map(one_block, block_ids)

    def column_pass(source_potential, previous):
        def advance(carry, index):
            maxima, totals = carry
            chosen = partners[index]
            scores = source_potential[index][None, :, None] - distances(sources[index], source_norms[index], targets[chosen], target_norms[chosen])
            mask = allowed[index][:, None, None]
            local_max = jnp.max(jnp.where(mask, scores, floor_value), axis=1)
            earlier = maxima[chosen]
            raised = jnp.maximum(earlier, local_max)
            partial_sum = jnp.sum(jnp.where(mask, jnp.exp(scores - raised[:, None, :]), 0.0), axis=1)
            totals = totals.at[chosen].set(totals[chosen] * jnp.exp(earlier - raised) + partial_sum)
            maxima = maxima.at[chosen].set(raised)
            return (maxima, totals), index
        start = (jnp.full((CLUSTER_BLOCKS, BS), floor_value, jnp.float32), jnp.zeros((CLUSTER_BLOCKS, BS), jnp.float32))
        (maxima, totals), leftover = lax.scan(advance, start, block_ids)
        reached = maxima > 0.5 * floor_value
        return jnp.where(reached, log_mass - (maxima + jnp.log(jnp.where(reached, totals, 1.0))), previous)

    potential = target_potential.reshape(CLUSTER_BLOCKS, BS)
    for sweep_index in range(SWEEPS):
        maxima, totals = row_pass(potential)
        source_side = log_mass - (maxima + jnp.log(totals))
        potential = column_pass(source_side, potential)
    maxima, totals = row_pass(potential)
    source_side = log_mass - (maxima + jnp.log(totals))

    def drift_block(index):
        chosen, scores = block_scores(index, potential)
        mask = allowed[index][:, None, None]
        weights = jnp.where(mask, jnp.exp(scores - maxima[index][None, :, None]), 0.0).astype(jnp.bfloat16)
        weights = weights.astype(jnp.float32)
        numerator = jnp.einsum("pij,pdj->di", weights, targets[chosen], precision=lax.Precision.HIGHEST)
        denominator = jnp.sum(weights, axis=(0, 2))
        return numerator / denominator[None, :] - sources[index]

    moved = lax.map(drift_block, block_ids)
    drift = jnp.transpose(moved, (1, 0, 2)).reshape(PC, NCELLS)
    return source_side.reshape(NCELLS), potential.reshape(NCELLS), drift
```

```python
import functools
import math

import jax
import jax.numpy as jnp
from jax import lax
from jax.experimental import pallas as pl
from jax.experimental.pallas import tpu as pltpu
from jax.sharding import PartitionSpec as P

SWEEPS = 2

floor_value = -1e30
PADDED = 32


def _slot_offsets(y_ref, g_ref, h_ref, ncomp):
    rows = lax.broadcasted_iota(jnp.int32, y_ref.shape[1:], 0)

    def one(t, c):
        yf = y_ref[t].astype(jnp.float32)
        sq = jnp.where(rows < ncomp, yf * yf, 0.0)
        ny = jnp.sum(sq, axis=0, keepdims=True)
        h_ref[t] = g_ref[t] - 0.25 * ny
        return c

    lax.fori_loop(0, y_ref.shape[0], one, 0)


def _row_scores(s, cnt, slots_ref, xs, y_ref, h_ref, s_ref, most, bs):
    def first(p, m):
        sl = slots_ref[s * most + p]
        prod = jnp.dot(xs, y_ref[sl], preferred_element_type=jnp.float32)
        sc = prod + h_ref[sl]
        s_ref[p] = sc
        return jnp.maximum(m, sc)

    m = lax.fori_loop(0, cnt, first, jnp.full((bs, bs), floor_value, jnp.float32))
    return jnp.max(m, axis=1, keepdims=True)


def sweep_kernel(slots_ref, counts_ref, xT_ref, y_ref, g_ref, amax_ref, asum_ref, h_ref, s_ref, *, most, log_mass, ncomp):
    nblk, bs = xT_ref.shape[0], xT_ref.shape[1]
    _slot_offsets(y_ref, g_ref, h_ref, ncomp)
    amax_ref[...] = jnp.full(amax_ref.shape, floor_value, jnp.float32)
    asum_ref[...] = jnp.zeros(asum_ref.shape, jnp.float32)

    def block(s, carry):
        cnt = counts_ref[s]
        xs = xT_ref[s]
        mrow = _row_scores(s, cnt, slots_ref, xs, y_ref, h_ref, s_ref, most, bs)
        mb = jnp.broadcast_to(mrow, (bs, bs))

        def second(p, acc):
            return acc + jnp.exp(s_ref[p] - mb)

        acc = lax.fori_loop(0, cnt, second, jnp.zeros((bs, bs), jnp.float32))
        tot = jnp.sum(acc, axis=1, keepdims=True)
        kb = jnp.broadcast_to(log_mass - (mrow + jnp.log(tot)), (bs, bs))

        def column(p, c):
            sl = slots_ref[s * most + p]
            v = s_ref[p] + kb
            cm = jnp.max(v, axis=0, keepdims=True)
            ce = jnp.sum(jnp.exp(v - cm), axis=0, keepdims=True)
            tm = cm - g_ref[sl]
            om = amax_ref[sl]
            nm = jnp.maximum(om, tm)
            asum_ref[sl] = asum_ref[sl] * jnp.exp(om - nm) + ce * jnp.exp(tm - nm)
            amax_ref[sl] = nm
            return c

        lax.fori_loop(0, cnt, column, 0)
        return carry

    lax.fori_loop(0, nblk, block, 0)


def final_kernel(slots_ref, counts_ref, xT_ref, x_ref, y_ref, g_ref, f_ref, drift_ref, h_ref, s_ref, *, most, log_mass, ncomp):
    nblk, bs = xT_ref.shape[0], xT_ref.shape[1]
    _slot_offsets(y_ref, g_ref, h_ref, ncomp)

    def block(s, carry):
        cnt = counts_ref[s]
        xs = xT_ref[s]
        mrow = _row_scores(s, cnt, slots_ref, xs, y_ref, h_ref, s_ref, most, bs)
        mb = jnp.broadcast_to(mrow, (bs, bs))

        def second(p, c):
            acc, num = c
            sl = slots_ref[s * most + p]
            e = jnp.exp(s_ref[p] - mb)
            w = e.astype(jnp.bfloat16)
            num = num + lax.dot_general(
                y_ref[sl], w, (((1,), (1,)), ((), ())), preferred_element_type=jnp.float32
            )
            return acc + e, num

        acc, num = lax.fori_loop(
            0,
            cnt,
            second,
            (jnp.zeros((bs, bs), jnp.float32), jnp.zeros((y_ref.shape[1], bs), jnp.float32)),
        )
        tot = jnp.sum(acc, axis=1, keepdims=True)
        xf = xs.astype(jnp.float32)
        quarter_nx = jnp.sum(xf * xf, axis=1, keepdims=True)
        fcol = log_mass - (mrow + jnp.log(tot)) + quarter_nx
        frow = jnp.transpose(jnp.broadcast_to(fcol, (bs, bs)))[0:1, :]
        f_ref[s] = frow
        off = pl.multiple_of(s * bs, bs)
        xcols = x_ref[:, pl.ds(off, bs)].astype(jnp.float32)
        drift_ref[:, pl.ds(off, bs)] = num[:ncomp] / num[ncomp : ncomp + 1] - xcols
        return carry

    lax.fori_loop(0, nblk, block, 0)


def _specs(kinds):
    return [pl.BlockSpec(memory_space=pltpu.SMEM if k == "s" else pltpu.VMEM) for k in kinds]


def local(source_coords, target_coords, target_potential, fetch_blocks, pair_slots, pair_counts):
    ncomp = source_coords.shape[0]
    nblk = pair_counts.shape[0]
    bs = source_coords.shape[1] // nblk
    peers = lax.axis_size("blocks")
    cap = fetch_blocks.shape[2]
    nslot = peers * cap
    most = pair_slots.shape[1]
    log_mass = -math.log(peers * nblk * bs)

    wanted = fetch_blocks[0]
    asked = lax.all_to_all(wanted, "blocks", split_axis=0, concat_axis=0, tiled=True)
    asked_local = (asked % nblk).reshape(-1)

    target_blocks = jnp.transpose(target_coords.reshape(ncomp, nblk, bs), (1, 0, 2))
    send_coords = target_blocks[asked_local].reshape(peers, cap, ncomp, bs)
    potential_here = target_potential.reshape(nblk, bs)
    send_potential = potential_here[asked_local].reshape(peers, cap, bs)
    came_coords = lax.all_to_all(send_coords, "blocks", split_axis=0, concat_axis=0, tiled=True)
    slot_potential = lax.all_to_all(send_potential, "blocks", split_axis=0, concat_axis=0, tiled=True)
    slot_potential = slot_potential.reshape(nslot, 1, bs)
    came_coords = came_coords.reshape(nslot, ncomp, bs)
    slot_coords = jnp.concatenate(
        [
            came_coords,
            jnp.ones((nslot, 1, bs), jnp.bfloat16),
            jnp.zeros((nslot, PADDED - ncomp - 1, bs), jnp.bfloat16),
        ],
        axis=1,
    )
    halved = (source_coords.astype(jnp.float32) * 0.5).astype(jnp.bfloat16)
    halved = jnp.concatenate([halved, jnp.zeros((PADDED - ncomp, nblk * bs), jnp.bfloat16)], axis=0)
    source_rows = jnp.transpose(halved.reshape(PADDED, nblk, bs), (1, 2, 0))
    flat_slots = pair_slots.reshape(-1)

    vmem = 48 * 1024 * 1024
    sweep = pl.pallas_call(
        functools.partial(sweep_kernel, most=most, log_mass=log_mass, ncomp=ncomp),
        out_shape=(jax.ShapeDtypeStruct((nslot, 1, bs), jnp.float32),) * 2,
        in_specs=_specs("ssvvv"),
        out_specs=tuple(_specs("vv")),
        scratch_shapes=[pltpu.VMEM((nslot, 1, bs), jnp.float32), pltpu.VMEM((most, bs, bs), jnp.float32)],
        compiler_params=pltpu.CompilerParams(vmem_limit_bytes=vmem),
    )
    final = pl.pallas_call(
        functools.partial(final_kernel, most=most, log_mass=log_mass, ncomp=ncomp),
        out_shape=(
            jax.ShapeDtypeStruct((nblk, 1, bs), jnp.float32),
            jax.ShapeDtypeStruct((ncomp, nblk * bs), jnp.float32),
        ),
        in_specs=_specs("ssvvvv"),
        out_specs=tuple(_specs("vv")),
        scratch_shapes=[pltpu.VMEM((nslot, 1, bs), jnp.float32), pltpu.VMEM((most, bs, bs), jnp.float32)],
        compiler_params=pltpu.CompilerParams(vmem_limit_bytes=vmem),
    )

    owned = asked_local[:, None] == jnp.arange(nblk, dtype=jnp.int32)[None, :]
    for sweep_index in range(SWEEPS):
        part_max, part_sum = sweep(flat_slots, pair_counts, source_rows, slot_coords, slot_potential)
        parts = jnp.stack([part_max.reshape(nslot, bs), part_sum.reshape(nslot, bs)], axis=1)
        came = lax.all_to_all(
            parts.reshape(peers, cap, 2, bs), "blocks", split_axis=0, concat_axis=0, tiled=True
        ).reshape(nslot, 2, bs)
        came_max = came[:, 0]
        came_sum = came[:, 1]
        merged = jnp.max(jnp.where(owned[:, :, None], came_max[:, None, :], floor_value), axis=0)
        scaled = came_sum[:, None, :] * jnp.exp(came_max[:, None, :] - merged[None, :, :])
        summed = jnp.sum(jnp.where(owned[:, :, None], scaled, 0.0), axis=0)
        reached = merged > 0.5 * floor_value
        potential_here = jnp.where(
            reached, log_mass - (merged + jnp.log(jnp.where(reached, summed, 1.0))), potential_here
        )
        send_potential = potential_here[asked_local].reshape(peers, cap, bs)
        slot_potential = lax.all_to_all(
            send_potential, "blocks", split_axis=0, concat_axis=0, tiled=True
        ).reshape(nslot, 1, bs)

    source_side, drift = final(flat_slots, pair_counts, source_rows, source_coords, slot_coords, slot_potential)
    return (source_side.reshape(-1), potential_here.reshape(-1), drift)


def solution(mesh):
    return jax.shard_map(
        local,
        mesh=mesh,
        in_specs=(
            P(None, ("groups", "blocks")),
            P(None, ("groups", "blocks")),
            P(("groups", "blocks")),
            P(("groups", "blocks"), None, None),
            P(("groups", "blocks"), None),
            P(("groups", "blocks")),
        ),
        out_specs=(P(("groups", "blocks")), P(("groups", "blocks")), P(None, ("groups", "blocks"))),
        check_vma=False,
    )
```

```python
import functools
import math

import jax
import jax.numpy as jnp
from jax import lax
from jax.experimental import pallas as pl
from jax.experimental.pallas import tpu as pltpu
from jax.sharding import PartitionSpec as P

SWEEPS = 2

floor_value = -1e30
PADDED = 32
CHUNK = 4


def _slot_offsets(y_ref, g_ref, h_ref, ncomp):
    rows = lax.broadcasted_iota(jnp.int32, y_ref.shape[1:], 0)

    def one(t, c):
        yf = y_ref[t].astype(jnp.float32)
        sq = jnp.where(rows < ncomp, yf * yf, 0.0)
        ny = jnp.sum(sq, axis=0, keepdims=True)
        h_ref[t] = g_ref[t] - 0.25 * ny
        return c

    lax.fori_loop(0, y_ref.shape[0], one, 0)


def _chunk_slots(slots_ref, s, q, most):
    return [slots_ref[s * most + jnp.minimum(q * CHUNK + c, most - 1)] for c in range(CHUNK)]


def _lane_fold(v, bs, op):
    out = v[:, 0:bs]
    for c in range(1, CHUNK):
        out = op(out, v[:, c * bs : (c + 1) * bs])
    return out


def _row_scores(s, cnt, slots_ref, xs, y_ref, h_ref, s_ref, most, bs):
    lane_tile = lax.broadcasted_iota(jnp.int32, (1, CHUNK * bs), 1) // bs

    def first(q, m):
        sls = _chunk_slots(slots_ref, s, q, most)
        rhs = jnp.concatenate([y_ref[sl] for sl in sls], axis=1)
        hrow = jnp.concatenate([h_ref[sl] for sl in sls], axis=1)
        prod = jnp.dot(xs, rhs, preferred_element_type=jnp.float32)
        sc = jnp.where(lane_tile + q * CHUNK < cnt, prod + hrow, floor_value)
        s_ref[q] = sc
        return jnp.maximum(m, _lane_fold(sc, bs, jnp.maximum))

    nq = (cnt + CHUNK - 1) // CHUNK
    m = lax.fori_loop(0, nq, first, jnp.full((bs, bs), floor_value, jnp.float32))
    return nq, jnp.max(m, axis=1, keepdims=True)


def sweep_kernel(slots_ref, counts_ref, xT_ref, y_ref, g_ref, amax_ref, asum_ref, h_ref, s_ref, *, most, log_mass, ncomp):
    nblk, bs = xT_ref.shape[0], xT_ref.shape[1]
    _slot_offsets(y_ref, g_ref, h_ref, ncomp)
    amax_ref[...] = jnp.full(amax_ref.shape, floor_value, jnp.float32)
    asum_ref[...] = jnp.zeros(asum_ref.shape, jnp.float32)

    def block(s, carry):
        cnt = counts_ref[s]
        nq, mrow = _row_scores(s, cnt, slots_ref, xT_ref[s], y_ref, h_ref, s_ref, most, bs)
        mb = jnp.concatenate([jnp.broadcast_to(mrow, (bs, bs))] * CHUNK, axis=1)

        def second(q, acc):
            return acc + _lane_fold(jnp.exp(s_ref[q] - mb), bs, jnp.add)

        acc = lax.fori_loop(0, nq, second, jnp.zeros((bs, bs), jnp.float32))
        tot = jnp.sum(acc, axis=1, keepdims=True)
        kb = jnp.concatenate([jnp.broadcast_to(log_mass - (mrow + jnp.log(tot)), (bs, bs))] * CHUNK, axis=1)

        def column(q, c):
            sls = _chunk_slots(slots_ref, s, q, most)
            v = s_ref[q] + kb
            cm = jnp.max(v, axis=0, keepdims=True)
            ce = jnp.sum(jnp.exp(v - cm), axis=0, keepdims=True)
            for t, sl in enumerate(sls):
                @pl.when(q * CHUNK + t < cnt)
                def _():
                    tm = cm[:, t * bs : (t + 1) * bs] - g_ref[sl]
                    om = amax_ref[sl]
                    nm = jnp.maximum(om, tm)
                    asum_ref[sl] = asum_ref[sl] * jnp.exp(om - nm) + ce[:, t * bs : (t + 1) * bs] * jnp.exp(tm - nm)
                    amax_ref[sl] = nm
            return c

        lax.fori_loop(0, nq, column, 0)
        return carry

    lax.fori_loop(0, nblk, block, 0)


def final_kernel(slots_ref, counts_ref, xT_ref, x_ref, y_ref, yT_ref, g_ref, f_ref, drift_ref, h_ref, s_ref, *, most, log_mass, ncomp):
    nblk, bs = xT_ref.shape[0], xT_ref.shape[1]
    _slot_offsets(y_ref, g_ref, h_ref, ncomp)
    lanes = lax.broadcasted_iota(jnp.int32, (bs, yT_ref.shape[2]), 1)

    def block(s, carry):
        cnt = counts_ref[s]
        xs = xT_ref[s]
        nq, mrow = _row_scores(s, cnt, slots_ref, xs, y_ref, h_ref, s_ref, most, bs)
        mb = jnp.concatenate([jnp.broadcast_to(mrow, (bs, bs))] * CHUNK, axis=1)

        def second(q, c):
            acc, num = c
            sls = _chunk_slots(slots_ref, s, q, most)
            e = jnp.exp(s_ref[q] - mb)
            w = e.astype(jnp.bfloat16)
            rhs = jnp.concatenate([yT_ref[sl] for sl in sls], axis=0)
            num = num + jnp.dot(w, rhs, preferred_element_type=jnp.float32)
            return acc + _lane_fold(e, bs, jnp.add), num

        acc, num = lax.fori_loop(
            0,
            nq,
            second,
            (jnp.zeros((bs, bs), jnp.float32), jnp.zeros((bs, yT_ref.shape[2]), jnp.float32)),
        )
        tot = jnp.sum(acc, axis=1, keepdims=True)
        xf = xs.astype(jnp.float32)
        quarter_nx = jnp.sum(xf * xf, axis=1, keepdims=True)
        fcol = log_mass - (mrow + jnp.log(tot)) + quarter_nx
        packed = jnp.where(lanes == PADDED - 1, jnp.broadcast_to(fcol, num.shape), num)
        rows = jnp.transpose(packed)
        f_ref[s] = rows[PADDED - 1 : PADDED, :]
        off = pl.multiple_of(s * bs, bs)
        xcols = x_ref[:, pl.ds(off, bs)].astype(jnp.float32)
        drift_ref[:, pl.ds(off, bs)] = rows[:ncomp] / rows[ncomp : ncomp + 1] - xcols
        return carry

    lax.fori_loop(0, nblk, block, 0)


def _specs(kinds):
    return [pl.BlockSpec(memory_space=pltpu.SMEM if k == "s" else pltpu.VMEM) for k in kinds]


def local(source_coords, target_coords, target_potential, fetch_blocks, pair_slots, pair_counts):
    ncomp = source_coords.shape[0]
    nblk = pair_counts.shape[0]
    bs = source_coords.shape[1] // nblk
    peers = lax.axis_size("blocks")
    cap = fetch_blocks.shape[2]
    nslot = peers * cap
    most = pair_slots.shape[1]
    log_mass = -math.log(peers * nblk * bs)
    chunks = (most + CHUNK - 1) // CHUNK

    wanted = fetch_blocks[0]
    asked = lax.all_to_all(wanted, "blocks", split_axis=0, concat_axis=0, tiled=True)
    asked_local = (asked % nblk).reshape(-1)

    potential_here = target_potential.reshape(nblk, bs)
    target_blocks = jnp.concatenate(
        [jnp.transpose(target_coords.reshape(ncomp, nblk, bs).astype(jnp.float32), (1, 0, 2)), potential_here[:, None, :]],
        axis=1,
    )
    send = target_blocks[asked_local].reshape(peers, cap, ncomp + 1, bs)
    came = lax.all_to_all(send, "blocks", split_axis=0, concat_axis=0, tiled=True).reshape(nslot, ncomp + 1, bs)
    slot_potential = came[:, ncomp:, :]
    came_coords = came[:, :ncomp, :].astype(jnp.bfloat16)
    slot_coords = jnp.concatenate(
        [
            came_coords,
            jnp.ones((nslot, 1, bs), jnp.bfloat16),
            jnp.zeros((nslot, PADDED - ncomp - 1, bs), jnp.bfloat16),
        ],
        axis=1,
    )
    slot_rows = jnp.concatenate(
        [jnp.transpose(slot_coords, (0, 2, 1)), jnp.zeros((nslot, bs, bs - PADDED), jnp.bfloat16)], axis=2
    )
    halved = (source_coords.astype(jnp.float32) * 0.5).astype(jnp.bfloat16)
    halved = jnp.concatenate([halved, jnp.zeros((PADDED - ncomp, nblk * bs), jnp.bfloat16)], axis=0)
    source_rows = jnp.transpose(halved.reshape(PADDED, nblk, bs), (1, 2, 0))
    flat_slots = pair_slots.reshape(-1)

    vmem = 48 * 1024 * 1024
    scratch = [pltpu.VMEM((nslot, 1, bs), jnp.float32), pltpu.VMEM((chunks, bs, CHUNK * bs), jnp.float32)]
    sweep = pl.pallas_call(
        functools.partial(sweep_kernel, most=most, log_mass=log_mass, ncomp=ncomp),
        out_shape=(jax.ShapeDtypeStruct((nslot, 1, bs), jnp.float32),) * 2,
        in_specs=_specs("ssvvv"),
        out_specs=tuple(_specs("vv")),
        scratch_shapes=scratch,
        compiler_params=pltpu.CompilerParams(vmem_limit_bytes=vmem),
    )
    final = pl.pallas_call(
        functools.partial(final_kernel, most=most, log_mass=log_mass, ncomp=ncomp),
        out_shape=(
            jax.ShapeDtypeStruct((nblk, 1, bs), jnp.float32),
            jax.ShapeDtypeStruct((ncomp, nblk * bs), jnp.float32),
        ),
        in_specs=_specs("ssvvvvv"),
        out_specs=tuple(_specs("vv")),
        scratch_shapes=scratch,
        compiler_params=pltpu.CompilerParams(vmem_limit_bytes=vmem),
    )

    owned = asked_local[:, None] == jnp.arange(nblk, dtype=jnp.int32)[None, :]
    for sweep_index in range(SWEEPS):
        part_max, part_sum = sweep(flat_slots, pair_counts, source_rows, slot_coords, slot_potential)
        parts = jnp.stack([part_max.reshape(nslot, bs), part_sum.reshape(nslot, bs)], axis=1)
        came = lax.all_to_all(
            parts.reshape(peers, cap, 2, bs), "blocks", split_axis=0, concat_axis=0, tiled=True
        ).reshape(nslot, 2, bs)
        came_max = came[:, 0]
        came_sum = came[:, 1]
        merged = jnp.max(jnp.where(owned[:, :, None], came_max[:, None, :], floor_value), axis=0)
        scaled = came_sum[:, None, :] * jnp.exp(came_max[:, None, :] - merged[None, :, :])
        summed = jnp.sum(jnp.where(owned[:, :, None], scaled, 0.0), axis=0)
        reached = merged > 0.5 * floor_value
        potential_here = jnp.where(
            reached, log_mass - (merged + jnp.log(jnp.where(reached, summed, 1.0))), potential_here
        )
        send_potential = potential_here[asked_local].reshape(peers, cap, bs)
        slot_potential = lax.all_to_all(
            send_potential, "blocks", split_axis=0, concat_axis=0, tiled=True
        ).reshape(nslot, 1, bs)

    source_side, drift = final(
        flat_slots, pair_counts, source_rows, source_coords, slot_coords, slot_rows, slot_potential
    )
    return (source_side.reshape(-1), potential_here.reshape(-1), drift)


def solution(mesh):
    return jax.shard_map(
        local,
        mesh=mesh,
        in_specs=(
            P(None, ("groups", "blocks")),
            P(None, ("groups", "blocks")),
            P(("groups", "blocks")),
            P(("groups", "blocks"), None, None),
            P(("groups", "blocks"), None),
            P(("groups", "blocks")),
        ),
        out_specs=(P(("groups", "blocks")), P(("groups", "blocks")), P(None, ("groups", "blocks"))),
        check_vma=False,
    )
```

```python
import functools
import math

import jax
import jax.numpy as jnp
from jax import lax
from jax.experimental import pallas as pl
from jax.experimental.pallas import tpu as pltpu
from jax.sharding import PartitionSpec as P

SWEEPS = 2

floor_value = -1e30
PADDED = 32
CHUNK = 8


def _slot_offsets(y_ref, g_ref, h_ref, ncomp):
    rows = lax.broadcasted_iota(jnp.int32, y_ref.shape[1:], 0)

    def one(t, c):
        yf = y_ref[t].astype(jnp.float32)
        sq = jnp.where(rows < ncomp, yf * yf, 0.0)
        ny = jnp.sum(sq, axis=0, keepdims=True)
        h_ref[t] = g_ref[t] - 0.25 * ny
        return c

    lax.fori_loop(0, y_ref.shape[0], one, 0)


def _chunk_slots(slots_ref, s, q, most):
    return [slots_ref[s * most + jnp.minimum(q * CHUNK + c, most - 1)] for c in range(CHUNK)]


def _lane_fold(v, bs, op):
    out = v[:, 0:bs]
    for c in range(1, CHUNK):
        out = op(out, v[:, c * bs : (c + 1) * bs])
    return out


def _row_scores(s, cnt, slots_ref, xs, y_ref, h_ref, s_ref, most, bs):
    lane_tile = lax.broadcasted_iota(jnp.int32, (1, CHUNK * bs), 1) // bs

    def first(q, m):
        sls = _chunk_slots(slots_ref, s, q, most)
        rhs = jnp.concatenate([y_ref[sl] for sl in sls], axis=1)
        hrow = jnp.concatenate([h_ref[sl] for sl in sls], axis=1)
        hrow = jnp.where(lane_tile + q * CHUNK < cnt, hrow, floor_value)
        sc = jnp.dot(xs, rhs, preferred_element_type=jnp.float32) + hrow
        s_ref[q] = sc
        return jnp.maximum(m, _lane_fold(sc, bs, jnp.maximum))

    nq = (cnt + CHUNK - 1) // CHUNK
    m = lax.fori_loop(0, nq, first, jnp.full((bs, bs), floor_value, jnp.float32))
    return nq, jnp.max(m, axis=1, keepdims=True)


def sweep_kernel(slots_ref, counts_ref, xT_ref, y_ref, g_ref, amax_ref, asum_ref, h_ref, s_ref, *, most, log_mass, ncomp):
    nblk, bs = xT_ref.shape[0], xT_ref.shape[1]
    _slot_offsets(y_ref, g_ref, h_ref, ncomp)
    amax_ref[...] = jnp.full(amax_ref.shape, floor_value, jnp.float32)
    asum_ref[...] = jnp.zeros(asum_ref.shape, jnp.float32)

    def block(s, carry):
        cnt = counts_ref[s]
        nq, mrow = _row_scores(s, cnt, slots_ref, xT_ref[s], y_ref, h_ref, s_ref, most, bs)
        mb = jnp.concatenate([jnp.broadcast_to(mrow, (bs, bs))] * CHUNK, axis=1)

        def second(q, acc):
            return acc + _lane_fold(jnp.exp(s_ref[q] - mb), bs, jnp.add)

        acc = lax.fori_loop(0, nq, second, jnp.zeros((bs, bs), jnp.float32))
        tot = jnp.sum(acc, axis=1, keepdims=True)
        kb = jnp.concatenate([jnp.broadcast_to(log_mass - (mrow + jnp.log(tot)), (bs, bs))] * CHUNK, axis=1)

        def column(q, c):
            sls = _chunk_slots(slots_ref, s, q, most)
            v = s_ref[q] + kb
            cm = jnp.max(v, axis=0, keepdims=True)
            ce = jnp.sum(jnp.exp(v - cm), axis=0, keepdims=True)
            for t, sl in enumerate(sls):
                valid = q * CHUNK + t < cnt
                tm = jnp.where(valid, cm[:, t * bs : (t + 1) * bs] - g_ref[sl], floor_value)
                te = jnp.where(valid, ce[:, t * bs : (t + 1) * bs], 0.0)
                om = amax_ref[sl]
                nm = jnp.maximum(om, tm)
                asum_ref[sl] = asum_ref[sl] * jnp.exp(om - nm) + te * jnp.exp(tm - nm)
                amax_ref[sl] = nm
            return c

        lax.fori_loop(0, nq, column, 0)
        return carry

    lax.fori_loop(0, nblk, block, 0)


def final_kernel(slots_ref, counts_ref, xT_ref, x_ref, y_ref, yT_ref, g_ref, f_ref, drift_ref, h_ref, s_ref, *, most, log_mass, ncomp):
    nblk, bs = xT_ref.shape[0], xT_ref.shape[1]
    _slot_offsets(y_ref, g_ref, h_ref, ncomp)
    lanes = lax.broadcasted_iota(jnp.int32, (bs, yT_ref.shape[2]), 1)

    def block(s, carry):
        cnt = counts_ref[s]
        xs = xT_ref[s]
        nq, mrow = _row_scores(s, cnt, slots_ref, xs, y_ref, h_ref, s_ref, most, bs)
        mb = jnp.concatenate([jnp.broadcast_to(mrow, (bs, bs))] * CHUNK, axis=1)

        def second(q, c):
            acc, num = c
            sls = _chunk_slots(slots_ref, s, q, most)
            e = jnp.exp(s_ref[q] - mb)
            w = e.astype(jnp.bfloat16)
            rhs = jnp.concatenate([yT_ref[sl] for sl in sls], axis=0)
            num = num + jnp.dot(w, rhs, preferred_element_type=jnp.float32)
            return acc + _lane_fold(e, bs, jnp.add), num

        acc, num = lax.fori_loop(
            0,
            nq,
            second,
            (jnp.zeros((bs, bs), jnp.float32), jnp.zeros((bs, yT_ref.shape[2]), jnp.float32)),
        )
        tot = jnp.sum(acc, axis=1, keepdims=True)
        xf = xs.astype(jnp.float32)
        quarter_nx = jnp.sum(xf * xf, axis=1, keepdims=True)
        fcol = log_mass - (mrow + jnp.log(tot)) + quarter_nx
        packed = jnp.where(lanes == PADDED - 1, jnp.broadcast_to(fcol, num.shape), num)
        rows = jnp.transpose(packed)
        f_ref[s] = rows[PADDED - 1 : PADDED, :]
        off = pl.multiple_of(s * bs, bs)
        xcols = x_ref[:, pl.ds(off, bs)].astype(jnp.float32)
        drift_ref[:, pl.ds(off, bs)] = rows[:ncomp] / rows[ncomp : ncomp + 1] - xcols
        return carry

    lax.fori_loop(0, nblk, block, 0)


def _specs(kinds):
    return [pl.BlockSpec(memory_space=pltpu.SMEM if k == "s" else pltpu.VMEM) for k in kinds]


def local(source_coords, target_coords, target_potential, fetch_blocks, pair_slots, pair_counts):
    ncomp = source_coords.shape[0]
    nblk = pair_counts.shape[0]
    bs = source_coords.shape[1] // nblk
    peers = lax.axis_size("blocks")
    cap = fetch_blocks.shape[2]
    nslot = peers * cap
    most = pair_slots.shape[1]
    log_mass = -math.log(peers * nblk * bs)
    chunks = (most + CHUNK - 1) // CHUNK

    wanted = fetch_blocks[0]
    asked = lax.all_to_all(wanted, "blocks", split_axis=0, concat_axis=0, tiled=True)
    asked_local = (asked % nblk).reshape(-1)

    potential_here = target_potential.reshape(nblk, bs)
    target_blocks = jnp.concatenate(
        [jnp.transpose(target_coords.reshape(ncomp, nblk, bs).astype(jnp.float32), (1, 0, 2)), potential_here[:, None, :]],
        axis=1,
    )
    send = target_blocks[asked_local].reshape(peers, cap, ncomp + 1, bs)
    came = lax.all_to_all(send, "blocks", split_axis=0, concat_axis=0, tiled=True).reshape(nslot, ncomp + 1, bs)
    slot_potential = came[:, ncomp:, :]
    came_coords = came[:, :ncomp, :].astype(jnp.bfloat16)
    slot_coords = jnp.concatenate(
        [
            came_coords,
            jnp.ones((nslot, 1, bs), jnp.bfloat16),
            jnp.zeros((nslot, PADDED - ncomp - 1, bs), jnp.bfloat16),
        ],
        axis=1,
    )
    slot_rows = jnp.concatenate(
        [jnp.transpose(slot_coords, (0, 2, 1)), jnp.zeros((nslot, bs, bs - PADDED), jnp.bfloat16)], axis=2
    )
    halved = (source_coords.astype(jnp.float32) * 0.5).astype(jnp.bfloat16)
    halved = jnp.concatenate([halved, jnp.zeros((PADDED - ncomp, nblk * bs), jnp.bfloat16)], axis=0)
    source_rows = jnp.transpose(halved.reshape(PADDED, nblk, bs), (1, 2, 0))
    flat_slots = pair_slots.reshape(-1)

    vmem = 48 * 1024 * 1024
    scratch = [pltpu.VMEM((nslot, 1, bs), jnp.float32), pltpu.VMEM((chunks, bs, CHUNK * bs), jnp.float32)]
    sweep = pl.pallas_call(
        functools.partial(sweep_kernel, most=most, log_mass=log_mass, ncomp=ncomp),
        out_shape=(jax.ShapeDtypeStruct((nslot, 1, bs), jnp.float32),) * 2,
        in_specs=_specs("ssvvv"),
        out_specs=tuple(_specs("vv")),
        scratch_shapes=scratch,
        compiler_params=pltpu.CompilerParams(vmem_limit_bytes=vmem),
    )
    final = pl.pallas_call(
        functools.partial(final_kernel, most=most, log_mass=log_mass, ncomp=ncomp),
        out_shape=(
            jax.ShapeDtypeStruct((nblk, 1, bs), jnp.float32),
            jax.ShapeDtypeStruct((ncomp, nblk * bs), jnp.float32),
        ),
        in_specs=_specs("ssvvvvv"),
        out_specs=tuple(_specs("vv")),
        scratch_shapes=scratch,
        compiler_params=pltpu.CompilerParams(vmem_limit_bytes=vmem),
    )

    owned = asked_local[:, None] == jnp.arange(nblk, dtype=jnp.int32)[None, :]
    for sweep_index in range(SWEEPS):
        part_max, part_sum = sweep(flat_slots, pair_counts, source_rows, slot_coords, slot_potential)
        parts = jnp.stack([part_max.reshape(nslot, bs), part_sum.reshape(nslot, bs)], axis=1)
        came = lax.all_to_all(
            parts.reshape(peers, cap, 2, bs), "blocks", split_axis=0, concat_axis=0, tiled=True
        ).reshape(nslot, 2, bs)
        came_max = came[:, 0]
        came_sum = came[:, 1]
        merged = jnp.max(jnp.where(owned[:, :, None], came_max[:, None, :], floor_value), axis=0)
        scaled = came_sum[:, None, :] * jnp.exp(came_max[:, None, :] - merged[None, :, :])
        summed = jnp.sum(jnp.where(owned[:, :, None], scaled, 0.0), axis=0)
        reached = merged > 0.5 * floor_value
        potential_here = jnp.where(
            reached, log_mass - (merged + jnp.log(jnp.where(reached, summed, 1.0))), potential_here
        )
        send_potential = potential_here[asked_local].reshape(peers, cap, bs)
        slot_potential = lax.all_to_all(
            send_potential, "blocks", split_axis=0, concat_axis=0, tiled=True
        ).reshape(nslot, 1, bs)

    source_side, drift = final(
        flat_slots, pair_counts, source_rows, source_coords, slot_coords, slot_rows, slot_potential
    )
    return (source_side.reshape(-1), potential_here.reshape(-1), drift)


def solution(mesh):
    return jax.shard_map(
        local,
        mesh=mesh,
        in_specs=(
            P(None, ("groups", "blocks")),
            P(None, ("groups", "blocks")),
            P(("groups", "blocks")),
            P(("groups", "blocks"), None, None),
            P(("groups", "blocks"), None),
            P(("groups", "blocks")),
        ),
        out_specs=(P(("groups", "blocks")), P(("groups", "blocks")), P(None, ("groups", "blocks"))),
        check_vma=False,
    )
```

```python
import functools
import math

import jax
import jax.numpy as jnp
from jax import lax
from jax.experimental import pallas as pl
from jax.experimental.pallas import tpu as pltpu
from jax.sharding import PartitionSpec as P

SWEEPS = 2

floor_value = -1e30
PADDED = 32
CHUNK = 8


def _slot_offsets(y_ref, g_ref, h_ref, ncomp):
    rows = lax.broadcasted_iota(jnp.int32, y_ref.shape[1:], 0)

    def one(t, c):
        yf = y_ref[t].astype(jnp.float32)
        sq = jnp.where(rows < ncomp, yf * yf, 0.0)
        ny = jnp.sum(sq, axis=0, keepdims=True)
        h_ref[t] = g_ref[t] - 0.25 * ny
        return c

    lax.fori_loop(0, y_ref.shape[0], one, 0)


def _chunk_slots(slots_ref, s, q, most):
    return [slots_ref[s * most + jnp.minimum(q * CHUNK + c, most - 1)] for c in range(CHUNK)]


def _rows_of(values):
    return jnp.concatenate(values, axis=0)


def _row_scores(s, cnt, slots_ref, xs, y_ref, h_ref, s_ref, most, bs):
    lane_tile = lax.broadcasted_iota(jnp.int32, (1, CHUNK * bs), 1) // bs

    def first(q, m):
        sls = _chunk_slots(slots_ref, s, q, most)
        rhs = jnp.concatenate([y_ref[sl] for sl in sls], axis=1)
        hrow = jnp.concatenate([h_ref[sl] for sl in sls], axis=1)
        hrow = jnp.where(lane_tile + q * CHUNK < cnt, hrow, floor_value)
        sc = jnp.dot(xs, rhs, preferred_element_type=jnp.float32) + hrow
        for t in range(CHUNK):
            tile = sc[:, t * bs : (t + 1) * bs]
            s_ref[q, :, t * bs : (t + 1) * bs] = tile
            m = jnp.maximum(m, tile)
        return m

    nq = (cnt + CHUNK - 1) // CHUNK
    m = lax.fori_loop(0, nq, first, jnp.full((bs, bs), floor_value, jnp.float32))
    return nq, jnp.max(m, axis=1, keepdims=True)


def sweep_kernel(slots_ref, counts_ref, xT_ref, y_ref, g_ref, amax_ref, asum_ref, h_ref, s_ref, *, most, log_mass, ncomp):
    nblk, bs = xT_ref.shape[0], xT_ref.shape[1]
    _slot_offsets(y_ref, g_ref, h_ref, ncomp)
    amax_ref[...] = jnp.full(amax_ref.shape, floor_value, jnp.float32)
    asum_ref[...] = jnp.zeros(asum_ref.shape, jnp.float32)
    tile_row = lax.broadcasted_iota(jnp.int32, (CHUNK, bs), 0)

    def block(s, carry):
        cnt = counts_ref[s]
        nq, mrow = _row_scores(s, cnt, slots_ref, xT_ref[s], y_ref, h_ref, s_ref, most, bs)
        mb = jnp.broadcast_to(mrow, (bs, bs))

        def second(q, acc):
            for t in range(CHUNK):
                acc = acc + jnp.exp(s_ref[q, :, t * bs : (t + 1) * bs] - mb)
            return acc

        acc = lax.fori_loop(0, nq, second, jnp.zeros((bs, bs), jnp.float32))
        tot = jnp.sum(acc, axis=1, keepdims=True)
        kb = jnp.broadcast_to(log_mass - (mrow + jnp.log(tot)), (bs, bs))

        def column(q, c):
            sls = _chunk_slots(slots_ref, s, q, most)
            cms, ces = [], []
            for t in range(CHUNK):
                v = s_ref[q, :, t * bs : (t + 1) * bs] + kb
                cm = jnp.max(v, axis=0, keepdims=True)
                cms.append(cm)
                ces.append(jnp.sum(jnp.exp(v - cm), axis=0, keepdims=True))
            valid = tile_row + q * CHUNK < cnt
            tm = jnp.where(valid, _rows_of(cms) - _rows_of([g_ref[sl] for sl in sls]), floor_value)
            te = jnp.where(valid, _rows_of(ces), 0.0)
            om = _rows_of([amax_ref[sl] for sl in sls])
            os = _rows_of([asum_ref[sl] for sl in sls])
            nm = jnp.maximum(om, tm)
            ns = os * jnp.exp(om - nm) + te * jnp.exp(tm - nm)
            for t, sl in enumerate(sls):
                amax_ref[sl] = nm[t : t + 1]
                asum_ref[sl] = ns[t : t + 1]
            return c

        lax.fori_loop(0, nq, column, 0)
        return carry

    lax.fori_loop(0, nblk, block, 0)


def final_kernel(slots_ref, counts_ref, xT_ref, x_ref, y_ref, yT_ref, g_ref, f_ref, drift_ref, h_ref, s_ref, *, most, log_mass, ncomp):
    nblk, bs = xT_ref.shape[0], xT_ref.shape[1]
    _slot_offsets(y_ref, g_ref, h_ref, ncomp)
    lanes = lax.broadcasted_iota(jnp.int32, (bs, yT_ref.shape[2]), 1)

    def block(s, carry):
        cnt = counts_ref[s]
        xs = xT_ref[s]
        nq, mrow = _row_scores(s, cnt, slots_ref, xs, y_ref, h_ref, s_ref, most, bs)
        mb = jnp.broadcast_to(mrow, (bs, bs))

        def second(q, c):
            acc, num = c
            sls = _chunk_slots(slots_ref, s, q, most)
            for t, sl in enumerate(sls):
                e = jnp.exp(s_ref[q, :, t * bs : (t + 1) * bs] - mb)
                acc = acc + e
                num = num + jnp.dot(e.astype(jnp.bfloat16), yT_ref[sl], preferred_element_type=jnp.float32)
            return acc, num

        acc, num = lax.fori_loop(
            0,
            nq,
            second,
            (jnp.zeros((bs, bs), jnp.float32), jnp.zeros((bs, yT_ref.shape[2]), jnp.float32)),
        )
        tot = jnp.sum(acc, axis=1, keepdims=True)
        xf = xs.astype(jnp.float32)
        quarter_nx = jnp.sum(xf * xf, axis=1, keepdims=True)
        fcol = log_mass - (mrow + jnp.log(tot)) + quarter_nx
        packed = jnp.where(lanes == PADDED - 1, jnp.broadcast_to(fcol, num.shape), num)
        rows = jnp.transpose(packed)
        f_ref[s] = rows[PADDED - 1 : PADDED, :]
        off = pl.multiple_of(s * bs, bs)
        xcols = x_ref[:, pl.ds(off, bs)].astype(jnp.float32)
        drift_ref[:, pl.ds(off, bs)] = rows[:ncomp] / rows[ncomp : ncomp + 1] - xcols
        return carry

    lax.fori_loop(0, nblk, block, 0)


def _specs(kinds):
    return [pl.BlockSpec(memory_space=pltpu.SMEM if k == "s" else pltpu.VMEM) for k in kinds]


def local(source_coords, target_coords, target_potential, fetch_blocks, pair_slots, pair_counts):
    ncomp = source_coords.shape[0]
    nblk = pair_counts.shape[0]
    bs = source_coords.shape[1] // nblk
    peers = lax.axis_size("blocks")
    cap = fetch_blocks.shape[2]
    nslot = peers * cap
    most = pair_slots.shape[1]
    log_mass = -math.log(peers * nblk * bs)
    chunks = most // CHUNK
    assert most % CHUNK == 0

    wanted = fetch_blocks[0]
    asked = lax.all_to_all(wanted, "blocks", split_axis=0, concat_axis=0, tiled=True)
    asked_local = (asked % nblk).reshape(-1)

    potential_here = target_potential.reshape(nblk, bs)
    target_blocks = jnp.concatenate(
        [jnp.transpose(target_coords.reshape(ncomp, nblk, bs).astype(jnp.float32), (1, 0, 2)), potential_here[:, None, :]],
        axis=1,
    )
    send = target_blocks[asked_local].reshape(peers, cap, ncomp + 1, bs)
    came = lax.all_to_all(send, "blocks", split_axis=0, concat_axis=0, tiled=True).reshape(nslot, ncomp + 1, bs)
    slot_potential = came[:, ncomp:, :]
    came_coords = came[:, :ncomp, :].astype(jnp.bfloat16)
    slot_coords = jnp.concatenate(
        [
            came_coords,
            jnp.ones((nslot, 1, bs), jnp.bfloat16),
            jnp.zeros((nslot, PADDED - ncomp - 1, bs), jnp.bfloat16),
        ],
        axis=1,
    )
    slot_rows = jnp.concatenate(
        [jnp.transpose(slot_coords, (0, 2, 1)), jnp.zeros((nslot, bs, bs - PADDED), jnp.bfloat16)], axis=2
    )
    halved = (source_coords.astype(jnp.float32) * 0.5).astype(jnp.bfloat16)
    halved = jnp.concatenate([halved, jnp.zeros((PADDED - ncomp, nblk * bs), jnp.bfloat16)], axis=0)
    source_rows = jnp.transpose(halved.reshape(PADDED, nblk, bs), (1, 2, 0))
    flat_slots = pair_slots.reshape(-1)

    vmem = 48 * 1024 * 1024
    scratch = [pltpu.VMEM((nslot, 1, bs), jnp.float32), pltpu.VMEM((chunks, bs, CHUNK * bs), jnp.float32)]
    sweep = pl.pallas_call(
        functools.partial(sweep_kernel, most=most, log_mass=log_mass, ncomp=ncomp),
        out_shape=(jax.ShapeDtypeStruct((nslot, 1, bs), jnp.float32),) * 2,
        in_specs=_specs("ssvvv"),
        out_specs=tuple(_specs("vv")),
        scratch_shapes=scratch,
        compiler_params=pltpu.CompilerParams(vmem_limit_bytes=vmem),
    )
    final = pl.pallas_call(
        functools.partial(final_kernel, most=most, log_mass=log_mass, ncomp=ncomp),
        out_shape=(
            jax.ShapeDtypeStruct((nblk, 1, bs), jnp.float32),
            jax.ShapeDtypeStruct((ncomp, nblk * bs), jnp.float32),
        ),
        in_specs=_specs("ssvvvvv"),
        out_specs=tuple(_specs("vv")),
        scratch_shapes=scratch,
        compiler_params=pltpu.CompilerParams(vmem_limit_bytes=vmem),
    )

    owned = asked_local[:, None] == jnp.arange(nblk, dtype=jnp.int32)[None, :]
    for sweep_index in range(SWEEPS):
        part_max, part_sum = sweep(flat_slots, pair_counts, source_rows, slot_coords, slot_potential)
        parts = jnp.stack([part_max.reshape(nslot, bs), part_sum.reshape(nslot, bs)], axis=1)
        came = lax.all_to_all(
            parts.reshape(peers, cap, 2, bs), "blocks", split_axis=0, concat_axis=0, tiled=True
        ).reshape(nslot, 2, bs)
        came_max = came[:, 0]
        came_sum = came[:, 1]
        merged = jnp.max(jnp.where(owned[:, :, None], came_max[:, None, :], floor_value), axis=0)
        scaled = came_sum[:, None, :] * jnp.exp(came_max[:, None, :] - merged[None, :, :])
        summed = jnp.sum(jnp.where(owned[:, :, None], scaled, 0.0), axis=0)
        reached = merged > 0.5 * floor_value
        potential_here = jnp.where(
            reached, log_mass - (merged + jnp.log(jnp.where(reached, summed, 1.0))), potential_here
        )
        send_potential = potential_here[asked_local].reshape(peers, cap, bs)
        slot_potential = lax.all_to_all(
            send_potential, "blocks", split_axis=0, concat_axis=0, tiled=True
        ).reshape(nslot, 1, bs)

    source_side, drift = final(
        flat_slots, pair_counts, source_rows, source_coords, slot_coords, slot_rows, slot_potential
    )
    return (source_side.reshape(-1), potential_here.reshape(-1), drift)


def solution(mesh):
    return jax.shard_map(
        local,
        mesh=mesh,
        in_specs=(
            P(None, ("groups", "blocks")),
            P(None, ("groups", "blocks")),
            P(("groups", "blocks")),
            P(("groups", "blocks"), None, None),
            P(("groups", "blocks"), None),
            P(("groups", "blocks")),
        ),
        out_specs=(P(("groups", "blocks")), P(("groups", "blocks")), P(None, ("groups", "blocks"))),
        check_vma=False,
    )
```

```python
import functools
import math

import jax
import jax.numpy as jnp
from jax import lax
from jax.experimental import pallas as pl
from jax.experimental.pallas import tpu as pltpu
from jax.sharding import PartitionSpec as P

SWEEPS = 2

floor_value = -1e30
PADDED = 32
CHUNK = 8


def _slot_offsets(y_ref, g_ref, h_ref, ncomp):
    rows = lax.broadcasted_iota(jnp.int32, y_ref.shape[1:], 0)

    def one(t, c):
        yf = y_ref[t].astype(jnp.float32)
        sq = jnp.where(rows < ncomp, yf * yf, 0.0)
        ny = jnp.sum(sq, axis=0, keepdims=True)
        h_ref[t] = g_ref[t] - 0.25 * ny
        return c

    lax.fori_loop(0, y_ref.shape[0], one, 0)


def _chunk_slots(slots_ref, s, q, most):
    return [slots_ref[s * most + jnp.minimum(q * CHUNK + c, most - 1)] for c in range(CHUNK)]


def _rows_of(values):
    return jnp.concatenate(values, axis=0)


def _row_scores(s, cnt, slots_ref, xs, y_ref, h_ref, s_ref, most, bs):
    lane_tile = lax.broadcasted_iota(jnp.int32, (1, CHUNK * bs), 1) // bs

    def first(q, m):
        sls = _chunk_slots(slots_ref, s, q, most)
        rhs = jnp.concatenate([y_ref[sl] for sl in sls], axis=1)
        hrow = jnp.concatenate([h_ref[sl] for sl in sls], axis=1)
        hrow = jnp.where(lane_tile + q * CHUNK < cnt, hrow, floor_value)
        sc = jnp.dot(xs, rhs, preferred_element_type=jnp.float32) + hrow
        for t in range(CHUNK):
            tile = sc[:, t * bs : (t + 1) * bs]
            s_ref[q, :, t * bs : (t + 1) * bs] = tile
            m = jnp.maximum(m, tile)
        return m

    nq = (cnt + CHUNK - 1) // CHUNK
    m = lax.fori_loop(0, nq, first, jnp.full((bs, bs), floor_value, jnp.float32))
    return nq, jnp.max(m, axis=1, keepdims=True)


def sweep_kernel(slots_ref, counts_ref, xT_ref, y_ref, g_ref, lse_ref, amax_ref, asum_ref, h_ref, s_ref, *, most, log_mass, ncomp):
    nblk, bs = xT_ref.shape[0], xT_ref.shape[1]
    _slot_offsets(y_ref, g_ref, h_ref, ncomp)
    amax_ref[...] = jnp.full(amax_ref.shape, floor_value, jnp.float32)
    asum_ref[...] = jnp.zeros(asum_ref.shape, jnp.float32)
    tile_row = lax.broadcasted_iota(jnp.int32, (CHUNK, bs), 0)

    def block(s, carry):
        cnt = counts_ref[s]
        nq, mrow = _row_scores(s, cnt, slots_ref, xT_ref[s], y_ref, h_ref, s_ref, most, bs)
        mb = jnp.broadcast_to(mrow, (bs, bs))

        def second(q, acc):
            for t in range(CHUNK):
                acc = acc + jnp.exp(s_ref[q, :, t * bs : (t + 1) * bs] - mb)
            return acc

        acc = lax.fori_loop(0, nq, second, jnp.zeros((bs, bs), jnp.float32))
        tot = jnp.sum(acc, axis=1, keepdims=True)
        kb = jnp.broadcast_to(log_mass - (mrow + jnp.log(tot)), (bs, bs))

        def column(q, c):
            sls = _chunk_slots(slots_ref, s, q, most)
            cms, ces = [], []
            for t in range(CHUNK):
                v = s_ref[q, :, t * bs : (t + 1) * bs] + kb
                cm = jnp.max(v, axis=0, keepdims=True)
                cms.append(cm)
                ces.append(jnp.sum(jnp.exp(v - cm), axis=0, keepdims=True))
            valid = tile_row + q * CHUNK < cnt
            tm = jnp.where(valid, _rows_of(cms) - _rows_of([g_ref[sl] for sl in sls]), floor_value)
            te = jnp.where(valid, _rows_of(ces), 0.0)
            om = _rows_of([amax_ref[sl] for sl in sls])
            os = _rows_of([asum_ref[sl] for sl in sls])
            nm = jnp.maximum(om, tm)
            ns = os * jnp.exp(om - nm) + te * jnp.exp(tm - nm)
            for t, sl in enumerate(sls):
                amax_ref[sl] = nm[t : t + 1]
                asum_ref[sl] = ns[t : t + 1]
            return c

        lax.fori_loop(0, nq, column, 0)
        return carry

    lax.fori_loop(0, nblk, block, 0)

    def finish(t, c):
        am = amax_ref[t]
        lse_ref[t] = jnp.where(am > 0.5 * floor_value, am + jnp.log(asum_ref[t]), floor_value)
        return c

    lax.fori_loop(0, lse_ref.shape[0], finish, 0)


def final_kernel(slots_ref, counts_ref, xT_ref, x_ref, y_ref, yT_ref, g_ref, f_ref, drift_ref, h_ref, s_ref, *, most, log_mass, ncomp):
    nblk, bs = xT_ref.shape[0], xT_ref.shape[1]
    _slot_offsets(y_ref, g_ref, h_ref, ncomp)
    lanes = lax.broadcasted_iota(jnp.int32, (bs, yT_ref.shape[2]), 1)

    def block(s, carry):
        cnt = counts_ref[s]
        xs = xT_ref[s]
        nq, mrow = _row_scores(s, cnt, slots_ref, xs, y_ref, h_ref, s_ref, most, bs)
        mb = jnp.broadcast_to(mrow, (bs, bs))

        def second(q, c):
            acc, num = c
            sls = _chunk_slots(slots_ref, s, q, most)
            for t, sl in enumerate(sls):
                e = jnp.exp(s_ref[q, :, t * bs : (t + 1) * bs] - mb)
                acc = acc + e
                num = num + jnp.dot(e.astype(jnp.bfloat16), yT_ref[sl], preferred_element_type=jnp.float32)
            return acc, num

        acc, num = lax.fori_loop(
            0,
            nq,
            second,
            (jnp.zeros((bs, bs), jnp.float32), jnp.zeros((bs, yT_ref.shape[2]), jnp.float32)),
        )
        tot = jnp.sum(acc, axis=1, keepdims=True)
        xf = xs.astype(jnp.float32)
        quarter_nx = jnp.sum(xf * xf, axis=1, keepdims=True)
        fcol = log_mass - (mrow + jnp.log(tot)) + quarter_nx
        packed = jnp.where(lanes == PADDED - 1, jnp.broadcast_to(fcol, num.shape), num)
        rows = jnp.transpose(packed)
        f_ref[s] = rows[PADDED - 1 : PADDED, :]
        off = pl.multiple_of(s * bs, bs)
        xcols = x_ref[:, pl.ds(off, bs)].astype(jnp.float32)
        drift_ref[:, pl.ds(off, bs)] = rows[:ncomp] / rows[ncomp : ncomp + 1] - xcols
        return carry

    lax.fori_loop(0, nblk, block, 0)


def _specs(kinds):
    return [pl.BlockSpec(memory_space=pltpu.SMEM if k == "s" else pltpu.VMEM) for k in kinds]


def local(source_coords, target_coords, target_potential, fetch_blocks, pair_slots, pair_counts):
    ncomp = source_coords.shape[0]
    nblk = pair_counts.shape[0]
    bs = source_coords.shape[1] // nblk
    peers = lax.axis_size("blocks")
    cap = fetch_blocks.shape[2]
    nslot = peers * cap
    most = pair_slots.shape[1]
    log_mass = -math.log(peers * nblk * bs)
    chunks = most // CHUNK
    assert most % CHUNK == 0

    wanted = fetch_blocks[0]
    me = lax.axis_index("blocks")
    fetch_all = lax.all_to_all(
        jnp.broadcast_to(wanted[None], (peers, peers, cap)), "blocks", split_axis=0, concat_axis=0, tiled=True
    )
    asked = lax.dynamic_index_in_dim(fetch_all, me, axis=1, keepdims=False)
    asked_local = (asked % nblk).reshape(-1)

    potential_here = target_potential.reshape(nblk, bs)
    target_blocks = jnp.concatenate(
        [jnp.transpose(target_coords.reshape(ncomp, nblk, bs).astype(jnp.float32), (1, 0, 2)), potential_here[:, None, :]],
        axis=1,
    )
    send = target_blocks[asked_local].reshape(peers, cap, ncomp + 1, bs)
    came = lax.all_to_all(send, "blocks", split_axis=0, concat_axis=0, tiled=True).reshape(nslot, ncomp + 1, bs)
    slot_potential = came[:, ncomp:, :]
    came_coords = came[:, :ncomp, :].astype(jnp.bfloat16)
    slot_coords = jnp.concatenate(
        [
            came_coords,
            jnp.ones((nslot, 1, bs), jnp.bfloat16),
            jnp.zeros((nslot, PADDED - ncomp - 1, bs), jnp.bfloat16),
        ],
        axis=1,
    )
    slot_rows = jnp.concatenate(
        [jnp.transpose(slot_coords, (0, 2, 1)), jnp.zeros((nslot, bs, bs - PADDED), jnp.bfloat16)], axis=2
    )
    halved = (source_coords.astype(jnp.float32) * 0.5).astype(jnp.bfloat16)
    halved = jnp.concatenate([halved, jnp.zeros((PADDED - ncomp, nblk * bs), jnp.bfloat16)], axis=0)
    source_rows = jnp.transpose(halved.reshape(PADDED, nblk, bs), (1, 2, 0))
    flat_slots = pair_slots.reshape(-1)

    vmem = 48 * 1024 * 1024
    scratch = [pltpu.VMEM((nslot, 1, bs), jnp.float32), pltpu.VMEM((chunks, bs, CHUNK * bs), jnp.float32)]
    sweep = pl.pallas_call(
        functools.partial(sweep_kernel, most=most, log_mass=log_mass, ncomp=ncomp),
        out_shape=jax.ShapeDtypeStruct((nslot, 1, bs), jnp.float32),
        in_specs=_specs("ssvvv"),
        out_specs=_specs("v")[0],
        scratch_shapes=[pltpu.VMEM((nslot, 1, bs), jnp.float32)] * 2 + scratch,
        compiler_params=pltpu.CompilerParams(vmem_limit_bytes=vmem),
    )
    final = pl.pallas_call(
        functools.partial(final_kernel, most=most, log_mass=log_mass, ncomp=ncomp),
        out_shape=(
            jax.ShapeDtypeStruct((nblk, 1, bs), jnp.float32),
            jax.ShapeDtypeStruct((ncomp, nblk * bs), jnp.float32),
        ),
        in_specs=_specs("ssvvvvv"),
        out_specs=tuple(_specs("vv")),
        scratch_shapes=scratch,
        compiler_params=pltpu.CompilerParams(vmem_limit_bytes=vmem),
    )

    def combine(values, match, previous, axes):
        merged = jnp.max(jnp.where(match, values, floor_value), axis=axes)
        summed = jnp.sum(jnp.where(match, jnp.exp(values - jnp.expand_dims(merged, axes)), 0.0), axis=axes)
        reached = merged > 0.5 * floor_value
        return jnp.where(reached, log_mass - (merged + jnp.log(jnp.where(reached, summed, 1.0))), previous)

    owned = (asked_local.reshape(peers, cap)[None] == jnp.arange(nblk, dtype=jnp.int32)[:, None, None])[..., None]
    gather_all = peers * nslot * bs * 4 <= (1 << 20)
    if gather_all:
        fetched = jnp.transpose(fetch_all, (1, 0, 2))[:, None, :, :] == wanted[:, :, None, None]
        fetched = fetched[..., None]
    for sweep_index in range(SWEEPS):
        lse = sweep(flat_slots, pair_counts, source_rows, slot_coords, slot_potential).reshape(nslot, bs)
        if gather_all:
            came = lax.all_to_all(
                jnp.broadcast_to(lse[None], (peers, nslot, bs)), "blocks", split_axis=0, concat_axis=0, tiled=True
            ).reshape(peers, peers, cap, bs)
            mine = lax.dynamic_index_in_dim(came, me, axis=1, keepdims=False)
            potential_here = combine(mine[None], owned, potential_here, (1, 2))
            by_owner = jnp.transpose(came, (1, 0, 2, 3))[:, None]
            slot_potential = combine(
                by_owner, fetched, slot_potential.reshape(peers, cap, bs), (2, 3)
            ).reshape(nslot, 1, bs)
        else:
            came = lax.all_to_all(
                lse.reshape(peers, cap, bs), "blocks", split_axis=0, concat_axis=0, tiled=True
            )
            potential_here = combine(came[None], owned, potential_here, (1, 2))
            send_potential = potential_here[asked_local].reshape(peers, cap, bs)
            slot_potential = lax.all_to_all(
                send_potential, "blocks", split_axis=0, concat_axis=0, tiled=True
            ).reshape(nslot, 1, bs)

    source_side, drift = final(
        flat_slots, pair_counts, source_rows, source_coords, slot_coords, slot_rows, slot_potential
    )
    return (source_side.reshape(-1), potential_here.reshape(-1), drift)


def solution(mesh):
    return jax.shard_map(
        local,
        mesh=mesh,
        in_specs=(
            P(None, ("groups", "blocks")),
            P(None, ("groups", "blocks")),
            P(("groups", "blocks")),
            P(("groups", "blocks"), None, None),
            P(("groups", "blocks"), None),
            P(("groups", "blocks")),
        ),
        out_specs=(P(("groups", "blocks")), P(("groups", "blocks")), P(None, ("groups", "blocks"))),
        check_vma=False,
    )
```

```python
import functools
import math

import jax
import jax.numpy as jnp
from jax import lax
from jax.experimental import pallas as pl
from jax.experimental.pallas import tpu as pltpu
from jax.sharding import PartitionSpec as P

SWEEPS = 2

floor_value = -1e30
PADDED = 32
CHUNK = 8


def _chunk_slots(slots_ref, s, q, most):
    return [slots_ref[s * most + jnp.minimum(q * CHUNK + c, most - 1)] for c in range(CHUNK)]


def _rows_of(values):
    return jnp.concatenate(values, axis=0)


def _row_scores(s, cnt, slots_ref, xs, y_ref, h_ref, s_ref, most, bs):
    lane_tile = lax.broadcasted_iota(jnp.int32, (1, CHUNK * bs), 1) // bs

    def first(q, m):
        sls = _chunk_slots(slots_ref, s, q, most)
        rhs = jnp.concatenate([y_ref[sl] for sl in sls], axis=1)
        hrow = jnp.concatenate([h_ref[sl] for sl in sls], axis=1)
        hrow = jnp.where(lane_tile + q * CHUNK < cnt, hrow, floor_value)
        sc = jnp.dot(xs, rhs, preferred_element_type=jnp.float32) + hrow
        for t in range(CHUNK):
            tile = sc[:, t * bs : (t + 1) * bs]
            s_ref[q, :, t * bs : (t + 1) * bs] = tile
            m = jnp.maximum(m, tile)
        return m

    nq = (cnt + CHUNK - 1) // CHUNK
    m = lax.fori_loop(0, nq, first, jnp.full((bs, bs), floor_value, jnp.float32))
    return nq, jnp.max(m, axis=1, keepdims=True)


def sweep_kernel(slots_ref, counts_ref, xT_ref, y_ref, h_ref, g_ref, lse_ref, amax_ref, asum_ref, s_ref, *, most, log_mass):
    nblk, bs = xT_ref.shape[0], xT_ref.shape[1]
    amax_ref[...] = jnp.full(amax_ref.shape, floor_value, jnp.float32)
    asum_ref[...] = jnp.zeros(asum_ref.shape, jnp.float32)
    tile_row = lax.broadcasted_iota(jnp.int32, (CHUNK, bs), 0)

    def block(s, carry):
        cnt = counts_ref[s]
        nq, mrow = _row_scores(s, cnt, slots_ref, xT_ref[s], y_ref, h_ref, s_ref, most, bs)
        mb = jnp.broadcast_to(mrow, (bs, bs))

        def second(q, acc):
            for t in range(CHUNK):
                acc = acc + jnp.exp(s_ref[q, :, t * bs : (t + 1) * bs] - mb)
            return acc

        acc = lax.fori_loop(0, nq, second, jnp.zeros((bs, bs), jnp.float32))
        tot = jnp.sum(acc, axis=1, keepdims=True)
        kb = jnp.broadcast_to(log_mass - (mrow + jnp.log(tot)), (bs, bs))

        def column(q, c):
            sls = _chunk_slots(slots_ref, s, q, most)
            cms, ces = [], []
            for t in range(CHUNK):
                v = s_ref[q, :, t * bs : (t + 1) * bs] + kb
                cm = jnp.max(v, axis=0, keepdims=True)
                cms.append(cm)
                ces.append(jnp.sum(jnp.exp(v - cm), axis=0, keepdims=True))
            valid = tile_row + q * CHUNK < cnt
            tm = jnp.where(valid, _rows_of(cms) - _rows_of([g_ref[sl] for sl in sls]), floor_value)
            te = jnp.where(valid, _rows_of(ces), 0.0)
            om = _rows_of([amax_ref[sl] for sl in sls])
            os = _rows_of([asum_ref[sl] for sl in sls])
            nm = jnp.maximum(om, tm)
            ns = os * jnp.exp(om - nm) + te * jnp.exp(tm - nm)
            for t, sl in enumerate(sls):
                amax_ref[sl] = nm[t : t + 1]
                asum_ref[sl] = ns[t : t + 1]
            return c

        lax.fori_loop(0, nq, column, 0)
        return carry

    lax.fori_loop(0, nblk, block, 0)

    am = amax_ref[...]
    lse_ref[...] = jnp.where(am > 0.5 * floor_value, am + jnp.log(asum_ref[...]), floor_value)


def final_kernel(slots_ref, counts_ref, xT_ref, x_ref, y_ref, yT_ref, h_ref, f_ref, drift_ref, s_ref, *, most, log_mass, ncomp):
    nblk, bs = xT_ref.shape[0], xT_ref.shape[1]
    lanes = lax.broadcasted_iota(jnp.int32, (bs, yT_ref.shape[2]), 1)

    def block(s, carry):
        cnt = counts_ref[s]
        xs = xT_ref[s]
        nq, mrow = _row_scores(s, cnt, slots_ref, xs, y_ref, h_ref, s_ref, most, bs)
        mb = jnp.broadcast_to(mrow, (bs, bs))

        def second(q, c):
            acc, num = c
            sls = _chunk_slots(slots_ref, s, q, most)
            for t, sl in enumerate(sls):
                e = jnp.exp(s_ref[q, :, t * bs : (t + 1) * bs] - mb)
                acc = acc + e
                num = num + jnp.dot(e.astype(jnp.bfloat16), yT_ref[sl], preferred_element_type=jnp.float32)
            return acc, num

        acc, num = lax.fori_loop(
            0,
            nq,
            second,
            (jnp.zeros((bs, bs), jnp.float32), jnp.zeros((bs, yT_ref.shape[2]), jnp.float32)),
        )
        tot = jnp.sum(acc, axis=1, keepdims=True)
        xf = xs.astype(jnp.float32)
        quarter_nx = jnp.sum(xf * xf, axis=1, keepdims=True)
        fcol = log_mass - (mrow + jnp.log(tot)) + quarter_nx
        packed = jnp.where(lanes == PADDED - 1, jnp.broadcast_to(fcol, num.shape), num)
        rows = jnp.transpose(packed)
        f_ref[s] = rows[PADDED - 1 : PADDED, :]
        off = pl.multiple_of(s * bs, bs)
        xcols = x_ref[:, pl.ds(off, bs)].astype(jnp.float32)
        drift_ref[:, pl.ds(off, bs)] = rows[:ncomp] / rows[ncomp : ncomp + 1] - xcols
        return carry

    lax.fori_loop(0, nblk, block, 0)


def _specs(kinds):
    return [pl.BlockSpec(memory_space=pltpu.SMEM if k == "s" else pltpu.VMEM) for k in kinds]


def local(source_coords, target_coords, target_potential, fetch_blocks, pair_slots, pair_counts):
    ncomp = source_coords.shape[0]
    nblk = pair_counts.shape[0]
    bs = source_coords.shape[1] // nblk
    peers = lax.axis_size("blocks")
    cap = fetch_blocks.shape[2]
    nslot = peers * cap
    most = pair_slots.shape[1]
    log_mass = -math.log(peers * nblk * bs)
    chunks = most // CHUNK
    assert most % CHUNK == 0

    wanted = fetch_blocks[0]
    me = lax.axis_index("blocks")
    fetch_all = lax.all_to_all(
        jnp.broadcast_to(wanted[None], (peers, peers, cap)), "blocks", split_axis=0, concat_axis=0, tiled=True
    )
    asked = lax.dynamic_index_in_dim(fetch_all, me, axis=1, keepdims=False)
    asked_local = (asked % nblk).reshape(-1)

    potential_here = target_potential.reshape(nblk, bs)
    high = potential_here.astype(jnp.bfloat16)
    rest = potential_here - high.astype(jnp.float32)
    middle = rest.astype(jnp.bfloat16)
    low = (rest - middle.astype(jnp.float32)).astype(jnp.bfloat16)
    target_blocks = jnp.concatenate(
        [jnp.transpose(target_coords.reshape(ncomp, nblk, bs), (1, 0, 2)), high[:, None], middle[:, None], low[:, None]],
        axis=1,
    )
    send = target_blocks[asked_local].reshape(peers, cap, ncomp + 3, bs)
    came = lax.all_to_all(send, "blocks", split_axis=0, concat_axis=0, tiled=True).reshape(nslot, ncomp + 3, bs)
    pieces = came[:, ncomp:, :].astype(jnp.float32)
    slot_potential = (pieces[:, 0:1] + pieces[:, 1:2]) + pieces[:, 2:3]
    came_coords = came[:, :ncomp, :]
    came_wide = came_coords.astype(jnp.float32)
    quarter_ny = 0.25 * jnp.sum(came_wide * came_wide, axis=1, keepdims=True)
    slot_coords = jnp.concatenate(
        [
            came_coords,
            jnp.ones((nslot, 1, bs), jnp.bfloat16),
            jnp.zeros((nslot, PADDED - ncomp - 1, bs), jnp.bfloat16),
        ],
        axis=1,
    )
    slot_rows = jnp.concatenate(
        [jnp.transpose(slot_coords, (0, 2, 1)), jnp.zeros((nslot, bs, bs - PADDED), jnp.bfloat16)], axis=2
    )
    halved = (source_coords.astype(jnp.float32) * 0.5).astype(jnp.bfloat16)
    halved = jnp.concatenate([halved, jnp.zeros((PADDED - ncomp, nblk * bs), jnp.bfloat16)], axis=0)
    source_rows = jnp.transpose(halved.reshape(PADDED, nblk, bs), (1, 2, 0))
    flat_slots = pair_slots.reshape(-1)

    vmem = 48 * 1024 * 1024
    scratch = [pltpu.VMEM((nslot, 1, bs), jnp.float32), pltpu.VMEM((chunks, bs, CHUNK * bs), jnp.float32)]
    sweep = pl.pallas_call(
        functools.partial(sweep_kernel, most=most, log_mass=log_mass),
        out_shape=jax.ShapeDtypeStruct((nslot, 1, bs), jnp.float32),
        in_specs=_specs("ssvvvv"),
        out_specs=_specs("v")[0],
        scratch_shapes=[pltpu.VMEM((nslot, 1, bs), jnp.float32)] * 2 + scratch[1:],
        compiler_params=pltpu.CompilerParams(vmem_limit_bytes=vmem),
    )
    final = pl.pallas_call(
        functools.partial(final_kernel, most=most, log_mass=log_mass, ncomp=ncomp),
        out_shape=(
            jax.ShapeDtypeStruct((nblk, 1, bs), jnp.float32),
            jax.ShapeDtypeStruct((ncomp, nblk * bs), jnp.float32),
        ),
        in_specs=_specs("ssvvvvv"),
        out_specs=tuple(_specs("vv")),
        scratch_shapes=scratch[1:],
        compiler_params=pltpu.CompilerParams(vmem_limit_bytes=vmem),
    )

    def combine(values, match, previous, axes):
        merged = jnp.max(jnp.where(match, values, floor_value), axis=axes)
        summed = jnp.sum(jnp.where(match, jnp.exp(values - jnp.expand_dims(merged, axes)), 0.0), axis=axes)
        reached = merged > 0.5 * floor_value
        return jnp.where(reached, log_mass - (merged + jnp.log(jnp.where(reached, summed, 1.0))), previous)

    owned = (asked_local.reshape(peers, cap)[None] == jnp.arange(nblk, dtype=jnp.int32)[:, None, None])[..., None]
    gather_all = peers * nslot * bs * 4 <= (1 << 20)
    if gather_all:
        fetched = jnp.transpose(fetch_all, (1, 0, 2))[:, None, :, :] == wanted[:, :, None, None]
        fetched = fetched[..., None]
    for sweep_index in range(SWEEPS):
        lse = sweep(
            flat_slots, pair_counts, source_rows, slot_coords, slot_potential - quarter_ny, slot_potential
        ).reshape(nslot, bs)
        if gather_all:
            came = lax.all_to_all(
                jnp.broadcast_to(lse[None], (peers, nslot, bs)), "blocks", split_axis=0, concat_axis=0, tiled=True
            ).reshape(peers, peers, cap, bs)
            mine = lax.dynamic_index_in_dim(came, me, axis=1, keepdims=False)
            potential_here = combine(mine[None], owned, potential_here, (1, 2))
            by_owner = jnp.transpose(came, (1, 0, 2, 3))[:, None]
            slot_potential = combine(
                by_owner, fetched, slot_potential.reshape(peers, cap, bs), (2, 3)
            ).reshape(nslot, 1, bs)
        else:
            came = lax.all_to_all(
                lse.reshape(peers, cap, bs), "blocks", split_axis=0, concat_axis=0, tiled=True
            )
            potential_here = combine(came[None], owned, potential_here, (1, 2))
            send_potential = potential_here[asked_local].reshape(peers, cap, bs)
            slot_potential = lax.all_to_all(
                send_potential, "blocks", split_axis=0, concat_axis=0, tiled=True
            ).reshape(nslot, 1, bs)

    source_side, drift = final(
        flat_slots, pair_counts, source_rows, source_coords, slot_coords, slot_rows, slot_potential - quarter_ny
    )
    return (source_side.reshape(-1), potential_here.reshape(-1), drift)


def solution(mesh):
    return jax.shard_map(
        local,
        mesh=mesh,
        in_specs=(
            P(None, ("groups", "blocks")),
            P(None, ("groups", "blocks")),
            P(("groups", "blocks")),
            P(("groups", "blocks"), None, None),
            P(("groups", "blocks"), None),
            P(("groups", "blocks")),
        ),
        out_specs=(P(("groups", "blocks")), P(("groups", "blocks")), P(None, ("groups", "blocks"))),
        check_vma=False,
    )
```

```python
import functools
import math

import jax
import jax.numpy as jnp
from jax import lax
from jax.experimental import pallas as pl
from jax.experimental.pallas import tpu as pltpu
from jax.sharding import PartitionSpec as P

SWEEPS = 2

floor_value = -1e30
PADDED = 32
CHUNK = 8


def _chunk_slots(slots_ref, s, q, most):
    return [slots_ref[s * most + jnp.minimum(q * CHUNK + c, most - 1)] for c in range(CHUNK)]


def _rows_of(values):
    return jnp.concatenate(values, axis=0)


def _row_scores(s, cnt, slots_ref, xs, y_ref, h_ref, s_ref, most, bs):
    lane_tile = lax.broadcasted_iota(jnp.int32, (1, CHUNK * bs), 1) // bs

    def first(q, m):
        sls = _chunk_slots(slots_ref, s, q, most)
        rhs = jnp.concatenate([y_ref[sl] for sl in sls], axis=1)
        hrow = jnp.concatenate([h_ref[sl] for sl in sls], axis=1)
        hrow = jnp.where(lane_tile + q * CHUNK < cnt, hrow, floor_value)
        sc = jnp.dot(xs, rhs, preferred_element_type=jnp.float32) + hrow
        for t in range(CHUNK):
            tile = sc[:, t * bs : (t + 1) * bs]
            s_ref[q, :, t * bs : (t + 1) * bs] = tile
            m = jnp.maximum(m, tile)
        return m

    nq = (cnt + CHUNK - 1) // CHUNK
    m = lax.fori_loop(0, nq, first, jnp.full((bs, bs), floor_value, jnp.float32))
    return nq, jnp.max(m, axis=1, keepdims=True)


def sweep_kernel(slots_ref, counts_ref, xT_ref, y_ref, h_ref, g_ref, lse_ref, amax_ref, asum_ref, s_ref, *, most, log_mass):
    nblk, bs = xT_ref.shape[0], xT_ref.shape[1]
    amax_ref[...] = jnp.full(amax_ref.shape, floor_value, jnp.float32)
    asum_ref[...] = jnp.zeros(asum_ref.shape, jnp.float32)
    tile_row = lax.broadcasted_iota(jnp.int32, (CHUNK, bs), 0)

    def block(s, carry):
        cnt = counts_ref[s]
        nq, mrow = _row_scores(s, cnt, slots_ref, xT_ref[s], y_ref, h_ref, s_ref, most, bs)
        mb = jnp.broadcast_to(mrow, (bs, bs))

        def second(q, acc):
            for t in range(CHUNK):
                acc = acc + jnp.exp(s_ref[q, :, t * bs : (t + 1) * bs] - mb)
            return acc

        acc = lax.fori_loop(0, nq, second, jnp.zeros((bs, bs), jnp.float32))
        tot = jnp.sum(acc, axis=1, keepdims=True)
        kb = jnp.broadcast_to(log_mass - (mrow + jnp.log(tot)), (bs, bs))

        def column(q, c):
            sls = _chunk_slots(slots_ref, s, q, most)
            cms, ces = [], []
            for t in range(CHUNK):
                v = s_ref[q, :, t * bs : (t + 1) * bs] + kb
                cm = jnp.max(v, axis=0, keepdims=True)
                cms.append(cm)
                ces.append(jnp.sum(jnp.exp(v - cm), axis=0, keepdims=True))
            valid = tile_row + q * CHUNK < cnt
            tm = jnp.where(valid, _rows_of(cms) - _rows_of([g_ref[sl] for sl in sls]), floor_value)
            te = jnp.where(valid, _rows_of(ces), 0.0)
            om = _rows_of([amax_ref[sl] for sl in sls])
            os = _rows_of([asum_ref[sl] for sl in sls])
            nm = jnp.maximum(om, tm)
            ns = os * jnp.exp(om - nm) + te * jnp.exp(tm - nm)
            for t, sl in enumerate(sls):
                amax_ref[sl] = nm[t : t + 1]
                asum_ref[sl] = ns[t : t + 1]
            return c

        lax.fori_loop(0, nq, column, 0)
        return carry

    lax.fori_loop(0, nblk, block, 0)

    am = amax_ref[...]
    lse_ref[...] = jnp.where(am > 0.5 * floor_value, am + jnp.log(asum_ref[...]), floor_value)


def final_kernel(slots_ref, counts_ref, xT_ref, x_ref, y_ref, yT_ref, h_ref, f_ref, drift_ref, s_ref, *, most, log_mass, ncomp):
    nblk, bs = xT_ref.shape[0], xT_ref.shape[1]
    lanes = lax.broadcasted_iota(jnp.int32, (bs, yT_ref.shape[2]), 1)

    def block(s, carry):
        cnt = counts_ref[s]
        xs = xT_ref[s]
        nq, mrow = _row_scores(s, cnt, slots_ref, xs, y_ref, h_ref, s_ref, most, bs)
        mb = jnp.broadcast_to(mrow, (bs, bs))

        def second(q, c):
            acc, num = c
            sls = _chunk_slots(slots_ref, s, q, most)
            for t, sl in enumerate(sls):
                e = jnp.exp(s_ref[q, :, t * bs : (t + 1) * bs] - mb)
                acc = acc + e
                num = num + jnp.dot(e.astype(jnp.bfloat16), yT_ref[sl], preferred_element_type=jnp.float32)
            return acc, num

        acc, num = lax.fori_loop(
            0,
            nq,
            second,
            (jnp.zeros((bs, bs), jnp.float32), jnp.zeros((bs, yT_ref.shape[2]), jnp.float32)),
        )
        tot = jnp.sum(acc, axis=1, keepdims=True)
        xf = xs.astype(jnp.float32)
        quarter_nx = jnp.sum(xf * xf, axis=1, keepdims=True)
        fcol = log_mass - (mrow + jnp.log(tot)) + quarter_nx
        packed = jnp.where(lanes == PADDED - 1, jnp.broadcast_to(fcol, num.shape), num)
        rows = jnp.transpose(packed)
        f_ref[s] = rows[PADDED - 1 : PADDED, :]
        off = pl.multiple_of(s * bs, bs)
        xcols = x_ref[:, pl.ds(off, bs)].astype(jnp.float32)
        drift_ref[:, pl.ds(off, bs)] = rows[:ncomp] / rows[ncomp : ncomp + 1] - xcols
        return carry

    lax.fori_loop(0, nblk, block, 0)


def _specs(kinds):
    return [pl.BlockSpec(memory_space=pltpu.SMEM if k == "s" else pltpu.VMEM) for k in kinds]


def local(source_coords, target_coords, target_potential, fetch_blocks, pair_slots, pair_counts):
    ncomp = source_coords.shape[0]
    nblk = pair_counts.shape[0]
    bs = source_coords.shape[1] // nblk
    peers = lax.axis_size("blocks")
    cap = fetch_blocks.shape[2]
    nslot = peers * cap
    most = pair_slots.shape[1]
    log_mass = -math.log(peers * nblk * bs)
    chunks = most // CHUNK
    assert most % CHUNK == 0

    wanted = fetch_blocks[0]
    me = lax.axis_index("blocks")
    fetch_all = lax.all_to_all(
        jnp.broadcast_to(wanted[None], (peers, peers, cap)), "blocks", split_axis=0, concat_axis=0, tiled=True
    )
    asked = lax.dynamic_index_in_dim(fetch_all, me, axis=1, keepdims=False)
    asked_local = (asked % nblk).reshape(-1)

    potential_here = target_potential.reshape(nblk, bs)
    high_wide = lax.reduce_precision(potential_here, exponent_bits=8, mantissa_bits=7)
    rest = potential_here - high_wide
    middle_wide = lax.reduce_precision(rest, exponent_bits=8, mantissa_bits=7)
    high = high_wide.astype(jnp.bfloat16)
    middle = middle_wide.astype(jnp.bfloat16)
    low = (rest - middle_wide).astype(jnp.bfloat16)
    target_blocks = jnp.concatenate(
        [jnp.transpose(target_coords.reshape(ncomp, nblk, bs), (1, 0, 2)), high[:, None], middle[:, None], low[:, None]],
        axis=1,
    )
    send = target_blocks[asked_local].reshape(peers, cap, ncomp + 3, bs)
    came = lax.all_to_all(send, "blocks", split_axis=0, concat_axis=0, tiled=True).reshape(nslot, ncomp + 3, bs)
    pieces = came[:, ncomp:, :].astype(jnp.float32)
    slot_potential = (pieces[:, 0:1] + pieces[:, 1:2]) + pieces[:, 2:3]
    came_coords = came[:, :ncomp, :]
    came_wide = came_coords.astype(jnp.float32)
    quarter_ny = 0.25 * jnp.sum(came_wide * came_wide, axis=1, keepdims=True)
    slot_coords = jnp.concatenate(
        [
            came_coords,
            jnp.ones((nslot, 1, bs), jnp.bfloat16),
            jnp.zeros((nslot, PADDED - ncomp - 1, bs), jnp.bfloat16),
        ],
        axis=1,
    )
    slot_rows = jnp.concatenate(
        [jnp.transpose(slot_coords, (0, 2, 1)), jnp.zeros((nslot, bs, bs - PADDED), jnp.bfloat16)], axis=2
    )
    halved = (source_coords.astype(jnp.float32) * 0.5).astype(jnp.bfloat16)
    halved = jnp.concatenate([halved, jnp.zeros((PADDED - ncomp, nblk * bs), jnp.bfloat16)], axis=0)
    source_rows = jnp.transpose(halved.reshape(PADDED, nblk, bs), (1, 2, 0))
    flat_slots = pair_slots.reshape(-1)

    vmem = 48 * 1024 * 1024
    scratch = [pltpu.VMEM((nslot, 1, bs), jnp.float32), pltpu.VMEM((chunks, bs, CHUNK * bs), jnp.float32)]
    sweep = pl.pallas_call(
        functools.partial(sweep_kernel, most=most, log_mass=log_mass),
        out_shape=jax.ShapeDtypeStruct((nslot, 1, bs), jnp.float32),
        in_specs=_specs("ssvvvv"),
        out_specs=_specs("v")[0],
        scratch_shapes=[pltpu.VMEM((nslot, 1, bs), jnp.float32)] * 2 + scratch[1:],
        compiler_params=pltpu.CompilerParams(vmem_limit_bytes=vmem),
    )
    final = pl.pallas_call(
        functools.partial(final_kernel, most=most, log_mass=log_mass, ncomp=ncomp),
        out_shape=(
            jax.ShapeDtypeStruct((nblk, 1, bs), jnp.float32),
            jax.ShapeDtypeStruct((ncomp, nblk * bs), jnp.float32),
        ),
        in_specs=_specs("ssvvvvv"),
        out_specs=tuple(_specs("vv")),
        scratch_shapes=scratch[1:],
        compiler_params=pltpu.CompilerParams(vmem_limit_bytes=vmem),
    )

    def combine(values, match, previous, axes):
        merged = jnp.max(jnp.where(match, values, floor_value), axis=axes)
        summed = jnp.sum(jnp.where(match, jnp.exp(values - jnp.expand_dims(merged, axes)), 0.0), axis=axes)
        reached = merged > 0.5 * floor_value
        return jnp.where(reached, log_mass - (merged + jnp.log(jnp.where(reached, summed, 1.0))), previous)

    owned = (asked_local.reshape(peers, cap)[None] == jnp.arange(nblk, dtype=jnp.int32)[:, None, None])[..., None]
    gather_all = peers * nslot * bs * 4 <= (1 << 20)
    if gather_all:
        fetched = jnp.transpose(fetch_all, (1, 0, 2))[:, None, :, :] == wanted[:, :, None, None]
        fetched = fetched[..., None]
    for sweep_index in range(SWEEPS):
        lse = sweep(
            flat_slots, pair_counts, source_rows, slot_coords, slot_potential - quarter_ny, slot_potential
        ).reshape(nslot, bs)
        if gather_all:
            came = lax.all_to_all(
                jnp.broadcast_to(lse[None], (peers, nslot, bs)), "blocks", split_axis=0, concat_axis=0, tiled=True
            ).reshape(peers, peers, cap, bs)
            mine = lax.dynamic_index_in_dim(came, me, axis=1, keepdims=False)
            potential_here = combine(mine[None], owned, potential_here, (1, 2))
            by_owner = jnp.transpose(came, (1, 0, 2, 3))[:, None]
            slot_potential = combine(
                by_owner, fetched, slot_potential.reshape(peers, cap, bs), (2, 3)
            ).reshape(nslot, 1, bs)
        else:
            came = lax.all_to_all(
                lse.reshape(peers, cap, bs), "blocks", split_axis=0, concat_axis=0, tiled=True
            )
            potential_here = combine(came[None], owned, potential_here, (1, 2))
            send_potential = potential_here[asked_local].reshape(peers, cap, bs)
            slot_potential = lax.all_to_all(
                send_potential, "blocks", split_axis=0, concat_axis=0, tiled=True
            ).reshape(nslot, 1, bs)

    source_side, drift = final(
        flat_slots, pair_counts, source_rows, source_coords, slot_coords, slot_rows, slot_potential - quarter_ny
    )
    return (source_side.reshape(-1), potential_here.reshape(-1), drift)


def solution(mesh):
    return jax.shard_map(
        local,
        mesh=mesh,
        in_specs=(
            P(None, ("groups", "blocks")),
            P(None, ("groups", "blocks")),
            P(("groups", "blocks")),
            P(("groups", "blocks"), None, None),
            P(("groups", "blocks"), None),
            P(("groups", "blocks")),
        ),
        out_specs=(P(("groups", "blocks")), P(("groups", "blocks")), P(None, ("groups", "blocks"))),
        check_vma=False,
    )
```

```python
import functools
import math

import jax
import jax.numpy as jnp
from jax import lax
from jax.experimental import pallas as pl
from jax.experimental.pallas import tpu as pltpu
from jax.sharding import PartitionSpec as P

SWEEPS = 2

floor_value = -1e30
PADDED = 32
CHUNK = 8


def _chunk_slots(slots_ref, s, q, most):
    return [slots_ref[s * most + jnp.minimum(q * CHUNK + c, most - 1)] for c in range(CHUNK)]


def _rows_of(values):
    return jnp.concatenate(values, axis=0)


def _row_scores(s, cnt, slots_ref, xs, y_ref, h_ref, s_ref, most, bs):
    def first(q, m):
        sls = _chunk_slots(slots_ref, s, q, most)
        for t, sl in enumerate(sls):
            hrow = jnp.where(q * CHUNK + t < cnt, h_ref[sl], floor_value)
            tile = jnp.dot(xs, y_ref[sl], preferred_element_type=jnp.float32) + hrow
            s_ref[q, :, t * bs : (t + 1) * bs] = tile
            m = jnp.maximum(m, tile)
        return m

    nq = (cnt + CHUNK - 1) // CHUNK
    m = lax.fori_loop(0, nq, first, jnp.full((bs, bs), floor_value, jnp.float32))
    return nq, jnp.max(m, axis=1, keepdims=True)


def sweep_kernel(slots_ref, counts_ref, xT_ref, y_ref, h_ref, g_ref, lse_ref, amax_ref, asum_ref, s_ref, *, most, log_mass):
    nblk, bs = xT_ref.shape[0], xT_ref.shape[1]
    amax_ref[...] = jnp.full(amax_ref.shape, floor_value, jnp.float32)
    asum_ref[...] = jnp.zeros(asum_ref.shape, jnp.float32)
    tile_row = lax.broadcasted_iota(jnp.int32, (CHUNK, bs), 0)

    def block(s, carry):
        cnt = counts_ref[s]
        nq, mrow = _row_scores(s, cnt, slots_ref, xT_ref[s], y_ref, h_ref, s_ref, most, bs)
        mb = jnp.broadcast_to(mrow, (bs, bs))

        def second(q, acc):
            for t in range(CHUNK):
                acc = acc + jnp.exp(s_ref[q, :, t * bs : (t + 1) * bs] - mb)
            return acc

        acc = lax.fori_loop(0, nq, second, jnp.zeros((bs, bs), jnp.float32))
        tot = jnp.sum(acc, axis=1, keepdims=True)
        kb = jnp.broadcast_to(log_mass - (mrow + jnp.log(tot)), (bs, bs))

        def column(q, c):
            sls = _chunk_slots(slots_ref, s, q, most)
            cms, ces = [], []
            for t in range(CHUNK):
                v = s_ref[q, :, t * bs : (t + 1) * bs] + kb
                cm = jnp.max(v, axis=0, keepdims=True)
                cms.append(cm)
                ces.append(jnp.sum(jnp.exp(v - cm), axis=0, keepdims=True))
            valid = tile_row + q * CHUNK < cnt
            tm = jnp.where(valid, _rows_of(cms) - _rows_of([g_ref[sl] for sl in sls]), floor_value)
            te = jnp.where(valid, _rows_of(ces), 0.0)
            om = _rows_of([amax_ref[sl] for sl in sls])
            os = _rows_of([asum_ref[sl] for sl in sls])
            nm = jnp.maximum(om, tm)
            ns = os * jnp.exp(om - nm) + te * jnp.exp(tm - nm)
            for t, sl in enumerate(sls):
                amax_ref[sl] = nm[t : t + 1]
                asum_ref[sl] = ns[t : t + 1]
            return c

        lax.fori_loop(0, nq, column, 0)
        return carry

    lax.fori_loop(0, nblk, block, 0)

    am = amax_ref[...]
    lse = jnp.where(am > 0.5 * floor_value, am + jnp.log(asum_ref[...]), floor_value)
    for d in range(lse_ref.shape[0]):
        lse_ref[d] = lse


def final_kernel(slots_ref, counts_ref, xT_ref, x_ref, y_ref, yT_ref, h_ref, f_ref, drift_ref, s_ref, *, most, log_mass, ncomp):
    nblk, bs = xT_ref.shape[0], xT_ref.shape[1]
    lanes = lax.broadcasted_iota(jnp.int32, (bs, yT_ref.shape[2]), 1)

    def block(s, carry):
        cnt = counts_ref[s]
        xs = xT_ref[s]
        nq, mrow = _row_scores(s, cnt, slots_ref, xs, y_ref, h_ref, s_ref, most, bs)
        mb = jnp.broadcast_to(mrow, (bs, bs))

        def second(q, c):
            acc, num = c
            sls = _chunk_slots(slots_ref, s, q, most)
            for t, sl in enumerate(sls):
                e = jnp.exp(s_ref[q, :, t * bs : (t + 1) * bs] - mb)
                acc = acc + e
                num = num + jnp.dot(e.astype(jnp.bfloat16), yT_ref[sl], preferred_element_type=jnp.float32)
            return acc, num

        acc, num = lax.fori_loop(
            0,
            nq,
            second,
            (jnp.zeros((bs, bs), jnp.float32), jnp.zeros((bs, yT_ref.shape[2]), jnp.float32)),
        )
        tot = jnp.sum(acc, axis=1, keepdims=True)
        xf = xs.astype(jnp.float32)
        quarter_nx = jnp.sum(xf * xf, axis=1, keepdims=True)
        fcol = log_mass - (mrow + jnp.log(tot)) + quarter_nx
        packed = jnp.where(lanes == PADDED - 1, jnp.broadcast_to(fcol, num.shape), num)
        rows = jnp.transpose(packed)
        f_ref[s] = rows[PADDED - 1 : PADDED, :]
        off = pl.multiple_of(s * bs, bs)
        xcols = x_ref[:, pl.ds(off, bs)].astype(jnp.float32)
        drift_ref[:, pl.ds(off, bs)] = rows[:ncomp] / rows[ncomp : ncomp + 1] - xcols
        return carry

    lax.fori_loop(0, nblk, block, 0)


def _specs(kinds):
    return [pl.BlockSpec(memory_space=pltpu.SMEM if k == "s" else pltpu.VMEM) for k in kinds]


def local(source_coords, target_coords, target_potential, fetch_blocks, pair_slots, pair_counts):
    ncomp = source_coords.shape[0]
    nblk = pair_counts.shape[0]
    bs = source_coords.shape[1] // nblk
    peers = lax.axis_size("blocks")
    cap = fetch_blocks.shape[2]
    nslot = peers * cap
    most = pair_slots.shape[1]
    log_mass = -math.log(peers * nblk * bs)
    chunks = most // CHUNK
    assert most % CHUNK == 0

    wanted = fetch_blocks[0]
    me = lax.axis_index("blocks")
    fetch_all = lax.all_to_all(
        jnp.broadcast_to(wanted[None], (peers, peers, cap)), "blocks", split_axis=0, concat_axis=0, tiled=True
    )
    asked = lax.dynamic_index_in_dim(fetch_all, me, axis=1, keepdims=False)
    asked_local = (asked % nblk).reshape(-1)

    potential_here = target_potential.reshape(nblk, bs)
    high_wide = lax.reduce_precision(potential_here, exponent_bits=8, mantissa_bits=7)
    rest = potential_here - high_wide
    middle_wide = lax.reduce_precision(rest, exponent_bits=8, mantissa_bits=7)
    high = high_wide.astype(jnp.bfloat16)
    middle = middle_wide.astype(jnp.bfloat16)
    low = (rest - middle_wide).astype(jnp.bfloat16)
    target_blocks = jnp.concatenate(
        [jnp.transpose(target_coords.reshape(ncomp, nblk, bs), (1, 0, 2)), high[:, None], middle[:, None], low[:, None]],
        axis=1,
    )
    send = target_blocks[asked_local].reshape(peers, cap, ncomp + 3, bs)
    came = lax.all_to_all(send, "blocks", split_axis=0, concat_axis=0, tiled=True).reshape(nslot, ncomp + 3, bs)
    pieces = came[:, ncomp:, :].astype(jnp.float32)
    slot_potential = (pieces[:, 0:1] + pieces[:, 1:2]) + pieces[:, 2:3]
    came_coords = came[:, :ncomp, :]
    came_wide = came_coords.astype(jnp.float32)
    quarter_ny = 0.25 * jnp.sum(came_wide * came_wide, axis=1, keepdims=True)
    slot_coords = jnp.concatenate(
        [
            came_coords,
            jnp.ones((nslot, 1, bs), jnp.bfloat16),
            jnp.zeros((nslot, PADDED - ncomp - 1, bs), jnp.bfloat16),
        ],
        axis=1,
    )
    slot_rows = jnp.concatenate(
        [jnp.transpose(slot_coords, (0, 2, 1)), jnp.zeros((nslot, bs, bs - PADDED), jnp.bfloat16)], axis=2
    )
    halved = (source_coords.astype(jnp.float32) * 0.5).astype(jnp.bfloat16)
    halved = jnp.concatenate([halved, jnp.zeros((PADDED - ncomp, nblk * bs), jnp.bfloat16)], axis=0)
    source_rows = jnp.transpose(halved.reshape(PADDED, nblk, bs), (1, 2, 0))
    flat_slots = pair_slots.reshape(-1)

    vmem = 48 * 1024 * 1024
    scratch = [pltpu.VMEM((nslot, 1, bs), jnp.float32), pltpu.VMEM((chunks, bs, CHUNK * bs), jnp.float32)]
    gather_all = peers * nslot * bs * 4 <= (1 << 20)
    copies = peers if gather_all else 1
    sweep = pl.pallas_call(
        functools.partial(sweep_kernel, most=most, log_mass=log_mass),
        out_shape=jax.ShapeDtypeStruct((copies, nslot, 1, bs), jnp.float32),
        in_specs=_specs("ssvvvv"),
        out_specs=_specs("v")[0],
        scratch_shapes=[pltpu.VMEM((nslot, 1, bs), jnp.float32)] * 2 + scratch[1:],
        compiler_params=pltpu.CompilerParams(vmem_limit_bytes=vmem),
    )
    final = pl.pallas_call(
        functools.partial(final_kernel, most=most, log_mass=log_mass, ncomp=ncomp),
        out_shape=(
            jax.ShapeDtypeStruct((nblk, 1, bs), jnp.float32),
            jax.ShapeDtypeStruct((ncomp, nblk * bs), jnp.float32),
        ),
        in_specs=_specs("ssvvvvv"),
        out_specs=tuple(_specs("vv")),
        scratch_shapes=scratch[1:],
        compiler_params=pltpu.CompilerParams(vmem_limit_bytes=vmem),
    )

    def combine(values, match, previous, axes):
        merged = jnp.max(jnp.where(match, values, floor_value), axis=axes)
        summed = jnp.sum(jnp.where(match, jnp.exp(values - jnp.expand_dims(merged, axes)), 0.0), axis=axes)
        reached = merged > 0.5 * floor_value
        return jnp.where(reached, log_mass - (merged + jnp.log(jnp.where(reached, summed, 1.0))), previous)

    owned = (asked_local.reshape(peers, cap)[None] == jnp.arange(nblk, dtype=jnp.int32)[:, None, None])[..., None]
    if gather_all:
        fetched = jnp.transpose(fetch_all, (1, 0, 2))[:, None, :, :] == wanted[:, :, None, None]
        fetched = fetched[..., None]
    for sweep_index in range(SWEEPS):
        lse = sweep(
            flat_slots, pair_counts, source_rows, slot_coords, slot_potential - quarter_ny, slot_potential
        )
        if gather_all:
            came = lax.all_to_all(lse, "blocks", split_axis=0, concat_axis=0, tiled=True).reshape(peers, peers, cap, bs)
            mine = lax.dynamic_index_in_dim(came, me, axis=1, keepdims=False)
            potential_here = combine(mine[None], owned, potential_here, (1, 2))
            by_owner = jnp.transpose(came, (1, 0, 2, 3))[:, None]
            slot_potential = combine(
                by_owner, fetched, slot_potential.reshape(peers, cap, bs), (2, 3)
            ).reshape(nslot, 1, bs)
        else:
            came = lax.all_to_all(
                lse.reshape(peers, cap, bs), "blocks", split_axis=0, concat_axis=0, tiled=True
            )
            potential_here = combine(came[None], owned, potential_here, (1, 2))
            send_potential = potential_here[asked_local].reshape(peers, cap, bs)
            slot_potential = lax.all_to_all(
                send_potential, "blocks", split_axis=0, concat_axis=0, tiled=True
            ).reshape(nslot, 1, bs)

    source_side, drift = final(
        flat_slots, pair_counts, source_rows, source_coords, slot_coords, slot_rows, slot_potential - quarter_ny
    )
    return (source_side.reshape(-1), potential_here.reshape(-1), drift)


def solution(mesh):
    return jax.shard_map(
        local,
        mesh=mesh,
        in_specs=(
            P(None, ("groups", "blocks")),
            P(None, ("groups", "blocks")),
            P(("groups", "blocks")),
            P(("groups", "blocks"), None, None),
            P(("groups", "blocks"), None),
            P(("groups", "blocks")),
        ),
        out_specs=(P(("groups", "blocks")), P(("groups", "blocks")), P(None, ("groups", "blocks"))),
        check_vma=False,
    )
```

```python
import functools
import math

import jax
import jax.numpy as jnp
from jax import lax
from jax.experimental import pallas as pl
from jax.experimental.pallas import tpu as pltpu
from jax.sharding import PartitionSpec as P

SWEEPS = 2

floor_value = -1e30
PADDED = 32
CHUNK = 8
LOG2E = 1.4426950408889634
LN2 = 0.6931471805599453


def _chunk_slots(slots_ref, s, q, most):
    return [slots_ref[s * most + jnp.minimum(q * CHUNK + c, most - 1)] for c in range(CHUNK)]


def _rows_of(values):
    return jnp.concatenate(values, axis=0)


def _row_scores(s, cnt, slots_ref, xs, y_ref, h_ref, s_ref, most, bs):
    def first(q, m):
        sls = _chunk_slots(slots_ref, s, q, most)
        for t, sl in enumerate(sls):
            hrow = jnp.where(q * CHUNK + t < cnt, h_ref[sl], floor_value)
            tile = (jnp.dot(xs, y_ref[sl], preferred_element_type=jnp.float32) + hrow) * LOG2E
            s_ref[q, :, t * bs : (t + 1) * bs] = tile
            m = jnp.maximum(m, tile)
        return m

    nq = (cnt + CHUNK - 1) // CHUNK
    m = lax.fori_loop(0, nq, first, jnp.full((bs, bs), floor_value, jnp.float32))
    return nq, jnp.max(m, axis=1, keepdims=True)


def sweep_kernel(slots_ref, counts_ref, xT_ref, y_ref, h_ref, g_ref, lse_ref, amax_ref, asum_ref, s_ref, *, most, log_mass):
    nblk, bs = xT_ref.shape[0], xT_ref.shape[1]
    amax_ref[...] = jnp.full(amax_ref.shape, floor_value, jnp.float32)
    asum_ref[...] = jnp.zeros(asum_ref.shape, jnp.float32)
    tile_row = lax.broadcasted_iota(jnp.int32, (CHUNK, bs), 0)

    def block(s, carry):
        cnt = counts_ref[s]
        nq, mrow = _row_scores(s, cnt, slots_ref, xT_ref[s], y_ref, h_ref, s_ref, most, bs)
        mb = jnp.broadcast_to(mrow, (bs, bs))

        def second(q, acc):
            for t in range(CHUNK):
                acc = acc + jnp.exp2(s_ref[q, :, t * bs : (t + 1) * bs] - mb)
            return acc

        acc = lax.fori_loop(0, nq, second, jnp.zeros((bs, bs), jnp.float32))
        tot = jnp.sum(acc, axis=1, keepdims=True)
        kb = jnp.broadcast_to((log_mass - (mrow * LN2 + jnp.log(tot))) * LOG2E, (bs, bs))

        def column(q, c):
            sls = _chunk_slots(slots_ref, s, q, most)
            cms, ces = [], []
            for t in range(CHUNK):
                v = s_ref[q, :, t * bs : (t + 1) * bs] + kb
                cm = jnp.max(v, axis=0, keepdims=True)
                cms.append(cm)
                ces.append(jnp.sum(jnp.exp2(v - cm), axis=0, keepdims=True))
            valid = tile_row + q * CHUNK < cnt
            tm = jnp.where(valid, _rows_of(cms) * LN2 - _rows_of([g_ref[sl] for sl in sls]), floor_value)
            te = jnp.where(valid, _rows_of(ces), 0.0)
            om = _rows_of([amax_ref[sl] for sl in sls])
            os = _rows_of([asum_ref[sl] for sl in sls])
            nm = jnp.maximum(om, tm)
            ns = os * jnp.exp(om - nm) + te * jnp.exp(tm - nm)
            for t, sl in enumerate(sls):
                amax_ref[sl] = nm[t : t + 1]
                asum_ref[sl] = ns[t : t + 1]
            return c

        lax.fori_loop(0, nq, column, 0)
        return carry

    lax.fori_loop(0, nblk, block, 0)

    am = amax_ref[...]
    lse = jnp.where(am > 0.5 * floor_value, am + jnp.log(asum_ref[...]), floor_value)
    for d in range(lse_ref.shape[0]):
        lse_ref[d] = lse


def final_kernel(slots_ref, counts_ref, xT_ref, x_ref, y_ref, yT_ref, h_ref, f_ref, drift_ref, s_ref, *, most, log_mass, ncomp):
    nblk, bs = xT_ref.shape[0], xT_ref.shape[1]
    lanes = lax.broadcasted_iota(jnp.int32, (bs, yT_ref.shape[2]), 1)

    def block(s, carry):
        cnt = counts_ref[s]
        xs = xT_ref[s]
        nq, mrow = _row_scores(s, cnt, slots_ref, xs, y_ref, h_ref, s_ref, most, bs)
        mb = jnp.broadcast_to(mrow, (bs, bs))

        def second(q, c):
            acc, num = c
            sls = _chunk_slots(slots_ref, s, q, most)
            for t, sl in enumerate(sls):
                e = jnp.exp2(s_ref[q, :, t * bs : (t + 1) * bs] - mb)
                acc = acc + e
                num = num + jnp.dot(e.astype(jnp.bfloat16), yT_ref[sl], preferred_element_type=jnp.float32)
            return acc, num

        acc, num = lax.fori_loop(
            0,
            nq,
            second,
            (jnp.zeros((bs, bs), jnp.float32), jnp.zeros((bs, yT_ref.shape[2]), jnp.float32)),
        )
        tot = jnp.sum(acc, axis=1, keepdims=True)
        xf = xs.astype(jnp.float32)
        quarter_nx = jnp.sum(xf * xf, axis=1, keepdims=True)
        fcol = log_mass - (mrow * LN2 + jnp.log(tot)) + quarter_nx
        packed = jnp.where(lanes == PADDED - 1, jnp.broadcast_to(fcol, num.shape), num)
        rows = jnp.transpose(packed)
        f_ref[s] = rows[PADDED - 1 : PADDED, :]
        off = pl.multiple_of(s * bs, bs)
        xcols = x_ref[:, pl.ds(off, bs)].astype(jnp.float32)
        drift_ref[:, pl.ds(off, bs)] = rows[:ncomp] / rows[ncomp : ncomp + 1] - xcols
        return carry

    lax.fori_loop(0, nblk, block, 0)


def _specs(kinds):
    return [pl.BlockSpec(memory_space=pltpu.SMEM if k == "s" else pltpu.VMEM) for k in kinds]


def local(source_coords, target_coords, target_potential, fetch_blocks, pair_slots, pair_counts):
    ncomp = source_coords.shape[0]
    nblk = pair_counts.shape[0]
    bs = source_coords.shape[1] // nblk
    peers = lax.axis_size("blocks")
    cap = fetch_blocks.shape[2]
    nslot = peers * cap
    most = pair_slots.shape[1]
    log_mass = -math.log(peers * nblk * bs)
    chunks = most // CHUNK
    assert most % CHUNK == 0

    wanted = fetch_blocks[0]
    me = lax.axis_index("blocks")
    fetch_all = lax.all_to_all(
        jnp.broadcast_to(wanted[None], (peers, peers, cap)), "blocks", split_axis=0, concat_axis=0, tiled=True
    )
    asked = lax.dynamic_index_in_dim(fetch_all, me, axis=1, keepdims=False)
    asked_local = (asked % nblk).reshape(-1)

    potential_here = target_potential.reshape(nblk, bs)
    high_wide = lax.reduce_precision(potential_here, exponent_bits=8, mantissa_bits=7)
    rest = potential_here - high_wide
    middle_wide = lax.reduce_precision(rest, exponent_bits=8, mantissa_bits=7)
    high = high_wide.astype(jnp.bfloat16)
    middle = middle_wide.astype(jnp.bfloat16)
    low = (rest - middle_wide).astype(jnp.bfloat16)
    target_blocks = jnp.concatenate(
        [jnp.transpose(target_coords.reshape(ncomp, nblk, bs), (1, 0, 2)), high[:, None], middle[:, None], low[:, None]],
        axis=1,
    )
    send = target_blocks[asked_local].reshape(peers, cap, ncomp + 3, bs)
    came = lax.all_to_all(send, "blocks", split_axis=0, concat_axis=0, tiled=True).reshape(nslot, ncomp + 3, bs)
    pieces = came[:, ncomp:, :].astype(jnp.float32)
    slot_potential = (pieces[:, 0:1] + pieces[:, 1:2]) + pieces[:, 2:3]
    came_coords = came[:, :ncomp, :]
    came_wide = came_coords.astype(jnp.float32)
    quarter_ny = 0.25 * jnp.sum(came_wide * came_wide, axis=1, keepdims=True)
    slot_coords = jnp.concatenate(
        [
            came_coords,
            jnp.ones((nslot, 1, bs), jnp.bfloat16),
            jnp.zeros((nslot, PADDED - ncomp - 1, bs), jnp.bfloat16),
        ],
        axis=1,
    )
    slot_rows = jnp.concatenate(
        [jnp.transpose(slot_coords, (0, 2, 1)), jnp.zeros((nslot, bs, bs - PADDED), jnp.bfloat16)], axis=2
    )
    halved = (source_coords.astype(jnp.float32) * 0.5).astype(jnp.bfloat16)
    halved = jnp.concatenate([halved, jnp.zeros((PADDED - ncomp, nblk * bs), jnp.bfloat16)], axis=0)
    source_rows = jnp.transpose(halved.reshape(PADDED, nblk, bs), (1, 2, 0))
    flat_slots = pair_slots.reshape(-1)

    vmem = 48 * 1024 * 1024
    scratch = [pltpu.VMEM((nslot, 1, bs), jnp.float32), pltpu.VMEM((chunks, bs, CHUNK * bs), jnp.float32)]
    gather_all = peers * nslot * bs * 4 <= (1 << 20)
    copies = peers if gather_all else 1
    sweep = pl.pallas_call(
        functools.partial(sweep_kernel, most=most, log_mass=log_mass),
        out_shape=jax.ShapeDtypeStruct((copies, nslot, 1, bs), jnp.float32),
        in_specs=_specs("ssvvvv"),
        out_specs=_specs("v")[0],
        scratch_shapes=[pltpu.VMEM((nslot, 1, bs), jnp.float32)] * 2 + scratch[1:],
        compiler_params=pltpu.CompilerParams(vmem_limit_bytes=vmem),
    )
    final = pl.pallas_call(
        functools.partial(final_kernel, most=most, log_mass=log_mass, ncomp=ncomp),
        out_shape=(
            jax.ShapeDtypeStruct((nblk, 1, bs), jnp.float32),
            jax.ShapeDtypeStruct((ncomp, nblk * bs), jnp.float32),
        ),
        in_specs=_specs("ssvvvvv"),
        out_specs=tuple(_specs("vv")),
        scratch_shapes=scratch[1:],
        compiler_params=pltpu.CompilerParams(vmem_limit_bytes=vmem),
    )

    def combine(values, match, previous, axes):
        merged = jnp.max(jnp.where(match, values, floor_value), axis=axes)
        summed = jnp.sum(jnp.where(match, jnp.exp(values - jnp.expand_dims(merged, axes)), 0.0), axis=axes)
        reached = merged > 0.5 * floor_value
        return jnp.where(reached, log_mass - (merged + jnp.log(jnp.where(reached, summed, 1.0))), previous)

    owned = (asked_local.reshape(peers, cap)[None] == jnp.arange(nblk, dtype=jnp.int32)[:, None, None])[..., None]
    if gather_all:
        fetched = jnp.transpose(fetch_all, (1, 0, 2))[:, None, :, :] == wanted[:, :, None, None]
        fetched = fetched[..., None]
    for sweep_index in range(SWEEPS):
        lse = sweep(
            flat_slots, pair_counts, source_rows, slot_coords, slot_potential - quarter_ny, slot_potential
        )
        if gather_all:
            came = lax.all_to_all(lse, "blocks", split_axis=0, concat_axis=0, tiled=True).reshape(peers, peers, cap, bs)
            mine = lax.dynamic_index_in_dim(came, me, axis=1, keepdims=False)
            potential_here = combine(mine[None], owned, potential_here, (1, 2))
            by_owner = jnp.transpose(came, (1, 0, 2, 3))[:, None]
            slot_potential = combine(
                by_owner, fetched, slot_potential.reshape(peers, cap, bs), (2, 3)
            ).reshape(nslot, 1, bs)
        else:
            came = lax.all_to_all(
                lse.reshape(peers, cap, bs), "blocks", split_axis=0, concat_axis=0, tiled=True
            )
            potential_here = combine(came[None], owned, potential_here, (1, 2))
            send_potential = potential_here[asked_local].reshape(peers, cap, bs)
            slot_potential = lax.all_to_all(
                send_potential, "blocks", split_axis=0, concat_axis=0, tiled=True
            ).reshape(nslot, 1, bs)

    source_side, drift = final(
        flat_slots, pair_counts, source_rows, source_coords, slot_coords, slot_rows, slot_potential - quarter_ny
    )
    return (source_side.reshape(-1), potential_here.reshape(-1), drift)


def solution(mesh):
    return jax.shard_map(
        local,
        mesh=mesh,
        in_specs=(
            P(None, ("groups", "blocks")),
            P(None, ("groups", "blocks")),
            P(("groups", "blocks")),
            P(("groups", "blocks"), None, None),
            P(("groups", "blocks"), None),
            P(("groups", "blocks")),
        ),
        out_specs=(P(("groups", "blocks")), P(("groups", "blocks")), P(None, ("groups", "blocks"))),
        check_vma=False,
    )
```

```python
import functools
import math

import jax
import jax.numpy as jnp
from jax import lax
from jax.experimental import pallas as pl
from jax.experimental.pallas import tpu as pltpu
from jax.sharding import PartitionSpec as P

SWEEPS = 2

floor_value = -1e30
PADDED = 32
CHUNK = 8
TAIL = 2
LOG2E = 1.4426950408889634
LN2 = 0.6931471805599453


def _pair_loop(cnt, body, carry):
    full = cnt // CHUNK
    carry = lax.fori_loop(0, full, lambda q, c: body(q * CHUNK, CHUNK, c), carry)
    rest = (cnt - full * CHUNK + TAIL - 1) // TAIL
    return lax.fori_loop(0, rest, lambda q, c: body(full * CHUNK + q * TAIL, TAIL, c), carry)


def _slots_at(slots_ref, s, p0, size, most):
    return [slots_ref[s * most + p0 + t] for t in range(size)]


def _rows_of(values):
    return jnp.concatenate(values, axis=0)


def _row_scores(s, cnt, slots_ref, xs, y_ref, h_ref, s_ref, most, bs):
    def first(p0, size, m):
        for t, sl in enumerate(_slots_at(slots_ref, s, p0, size, most)):
            hrow = jnp.where(p0 + t < cnt, h_ref[sl], floor_value)
            tile = (jnp.dot(xs, y_ref[sl], preferred_element_type=jnp.float32) + hrow) * LOG2E
            s_ref[p0 + t] = tile
            m = jnp.maximum(m, tile)
        return m

    m = _pair_loop(cnt, first, jnp.full((bs, bs), floor_value, jnp.float32))
    return jnp.max(m, axis=1, keepdims=True)


def sweep_kernel(slots_ref, counts_ref, xT_ref, y_ref, h_ref, g_ref, lse_ref, amax_ref, asum_ref, s_ref, *, most, log_mass):
    nblk, bs = xT_ref.shape[0], xT_ref.shape[1]
    amax_ref[...] = jnp.full(amax_ref.shape, floor_value, jnp.float32)
    asum_ref[...] = jnp.zeros(asum_ref.shape, jnp.float32)

    def block(s, carry):
        cnt = counts_ref[s]
        mrow = _row_scores(s, cnt, slots_ref, xT_ref[s], y_ref, h_ref, s_ref, most, bs)
        mb = jnp.broadcast_to(mrow, (bs, bs))

        def second(p0, size, acc):
            for t in range(size):
                acc = acc + jnp.exp2(s_ref[p0 + t] - mb)
            return acc

        acc = _pair_loop(cnt, second, jnp.zeros((bs, bs), jnp.float32))
        tot = jnp.sum(acc, axis=1, keepdims=True)
        kb = jnp.broadcast_to((log_mass - (mrow * LN2 + jnp.log(tot))) * LOG2E, (bs, bs))

        def column(p0, size, c):
            sls = _slots_at(slots_ref, s, p0, size, most)
            cms, ces = [], []
            for t in range(size):
                v = s_ref[p0 + t] + kb
                cm = jnp.max(v, axis=0, keepdims=True)
                cms.append(cm)
                ces.append(jnp.sum(jnp.exp2(v - cm), axis=0, keepdims=True))
            valid = lax.broadcasted_iota(jnp.int32, (size, bs), 0) + p0 < cnt
            tm = jnp.where(valid, _rows_of(cms) * LN2 - _rows_of([g_ref[sl] for sl in sls]), floor_value)
            te = jnp.where(valid, _rows_of(ces), 0.0)
            om = _rows_of([amax_ref[sl] for sl in sls])
            os = _rows_of([asum_ref[sl] for sl in sls])
            nm = jnp.maximum(om, tm)
            ns = os * jnp.exp(om - nm) + te * jnp.exp(tm - nm)
            for t, sl in enumerate(sls):
                amax_ref[sl] = nm[t : t + 1]
                asum_ref[sl] = ns[t : t + 1]
            return c

        _pair_loop(cnt, column, 0)
        return carry

    lax.fori_loop(0, nblk, block, 0)

    am = amax_ref[...]
    lse = jnp.where(am > 0.5 * floor_value, am + jnp.log(asum_ref[...]), floor_value)
    for d in range(lse_ref.shape[0]):
        lse_ref[d] = lse


def final_kernel(slots_ref, counts_ref, xT_ref, x_ref, y_ref, yT_ref, h_ref, f_ref, drift_ref, s_ref, *, most, log_mass, ncomp):
    nblk, bs = xT_ref.shape[0], xT_ref.shape[1]
    lanes = lax.broadcasted_iota(jnp.int32, (bs, yT_ref.shape[2]), 1)

    def block(s, carry):
        cnt = counts_ref[s]
        xs = xT_ref[s]
        mrow = _row_scores(s, cnt, slots_ref, xs, y_ref, h_ref, s_ref, most, bs)
        mb = jnp.broadcast_to(mrow, (bs, bs))

        def second(p0, size, c):
            acc, num = c
            for t, sl in enumerate(_slots_at(slots_ref, s, p0, size, most)):
                e = jnp.exp2(s_ref[p0 + t] - mb)
                acc = acc + e
                num = num + jnp.dot(e.astype(jnp.bfloat16), yT_ref[sl], preferred_element_type=jnp.float32)
            return acc, num

        acc, num = _pair_loop(
            cnt, second, (jnp.zeros((bs, bs), jnp.float32), jnp.zeros((bs, yT_ref.shape[2]), jnp.float32))
        )
        tot = jnp.sum(acc, axis=1, keepdims=True)
        xf = xs.astype(jnp.float32)
        quarter_nx = jnp.sum(xf * xf, axis=1, keepdims=True)
        fcol = log_mass - (mrow * LN2 + jnp.log(tot)) + quarter_nx
        packed = jnp.where(lanes == PADDED - 1, jnp.broadcast_to(fcol, num.shape), num)
        rows = jnp.transpose(packed)
        f_ref[s] = rows[PADDED - 1 : PADDED, :]
        off = pl.multiple_of(s * bs, bs)
        xcols = x_ref[:, pl.ds(off, bs)].astype(jnp.float32)
        drift_ref[:, pl.ds(off, bs)] = rows[:ncomp] / rows[ncomp : ncomp + 1] - xcols
        return carry

    lax.fori_loop(0, nblk, block, 0)


def _specs(kinds):
    return [pl.BlockSpec(memory_space=pltpu.SMEM if k == "s" else pltpu.VMEM) for k in kinds]


def local(source_coords, target_coords, target_potential, fetch_blocks, pair_slots, pair_counts):
    ncomp = source_coords.shape[0]
    nblk = pair_counts.shape[0]
    bs = source_coords.shape[1] // nblk
    peers = lax.axis_size("blocks")
    cap = fetch_blocks.shape[2]
    nslot = peers * cap
    most = pair_slots.shape[1]
    log_mass = -math.log(peers * nblk * bs)
    assert most % TAIL == 0

    wanted = fetch_blocks[0]
    me = lax.axis_index("blocks")
    fetch_all = lax.all_to_all(
        jnp.broadcast_to(wanted[None], (peers, peers, cap)), "blocks", split_axis=0, concat_axis=0, tiled=True
    )
    asked = lax.dynamic_index_in_dim(fetch_all, me, axis=1, keepdims=False)
    asked_local = (asked % nblk).reshape(-1)

    potential_here = target_potential.reshape(nblk, bs)
    high_wide = lax.reduce_precision(potential_here, exponent_bits=8, mantissa_bits=7)
    rest = potential_here - high_wide
    middle_wide = lax.reduce_precision(rest, exponent_bits=8, mantissa_bits=7)
    high = high_wide.astype(jnp.bfloat16)
    middle = middle_wide.astype(jnp.bfloat16)
    low = (rest - middle_wide).astype(jnp.bfloat16)
    target_blocks = jnp.concatenate(
        [jnp.transpose(target_coords.reshape(ncomp, nblk, bs), (1, 0, 2)), high[:, None], middle[:, None], low[:, None]],
        axis=1,
    )
    send = target_blocks[asked_local].reshape(peers, cap, ncomp + 3, bs)
    came = lax.all_to_all(send, "blocks", split_axis=0, concat_axis=0, tiled=True).reshape(nslot, ncomp + 3, bs)
    pieces = came[:, ncomp:, :].astype(jnp.float32)
    slot_potential = (pieces[:, 0:1] + pieces[:, 1:2]) + pieces[:, 2:3]
    came_coords = came[:, :ncomp, :]
    came_wide = came_coords.astype(jnp.float32)
    quarter_ny = 0.25 * jnp.sum(came_wide * came_wide, axis=1, keepdims=True)
    slot_coords = jnp.concatenate(
        [
            came_coords,
            jnp.ones((nslot, 1, bs), jnp.bfloat16),
            jnp.zeros((nslot, PADDED - ncomp - 1, bs), jnp.bfloat16),
        ],
        axis=1,
    )
    slot_rows = jnp.concatenate(
        [jnp.transpose(slot_coords, (0, 2, 1)), jnp.zeros((nslot, bs, bs - PADDED), jnp.bfloat16)], axis=2
    )
    halved = (source_coords.astype(jnp.float32) * 0.5).astype(jnp.bfloat16)
    halved = jnp.concatenate([halved, jnp.zeros((PADDED - ncomp, nblk * bs), jnp.bfloat16)], axis=0)
    source_rows = jnp.transpose(halved.reshape(PADDED, nblk, bs), (1, 2, 0))
    flat_slots = pair_slots.reshape(-1)

    vmem = 48 * 1024 * 1024
    scratch = [pltpu.VMEM((nslot, 1, bs), jnp.float32), pltpu.VMEM((most, bs, bs), jnp.float32)]
    gather_all = peers * nslot * bs * 4 <= (1 << 20)
    copies = peers if gather_all else 1
    sweep = pl.pallas_call(
        functools.partial(sweep_kernel, most=most, log_mass=log_mass),
        out_shape=jax.ShapeDtypeStruct((copies, nslot, 1, bs), jnp.float32),
        in_specs=_specs("ssvvvv"),
        out_specs=_specs("v")[0],
        scratch_shapes=[pltpu.VMEM((nslot, 1, bs), jnp.float32)] * 2 + scratch[1:],
        compiler_params=pltpu.CompilerParams(vmem_limit_bytes=vmem),
    )
    final = pl.pallas_call(
        functools.partial(final_kernel, most=most, log_mass=log_mass, ncomp=ncomp),
        out_shape=(
            jax.ShapeDtypeStruct((nblk, 1, bs), jnp.float32),
            jax.ShapeDtypeStruct((ncomp, nblk * bs), jnp.float32),
        ),
        in_specs=_specs("ssvvvvv"),
        out_specs=tuple(_specs("vv")),
        scratch_shapes=scratch[1:],
        compiler_params=pltpu.CompilerParams(vmem_limit_bytes=vmem),
    )

    def combine(values, match, previous, axes):
        merged = jnp.max(jnp.where(match, values, floor_value), axis=axes)
        summed = jnp.sum(jnp.where(match, jnp.exp(values - jnp.expand_dims(merged, axes)), 0.0), axis=axes)
        reached = merged > 0.5 * floor_value
        return jnp.where(reached, log_mass - (merged + jnp.log(jnp.where(reached, summed, 1.0))), previous)

    owned = (asked_local.reshape(peers, cap)[None] == jnp.arange(nblk, dtype=jnp.int32)[:, None, None])[..., None]
    if gather_all:
        fetched = jnp.transpose(fetch_all, (1, 0, 2))[:, None, :, :] == wanted[:, :, None, None]
        fetched = fetched[..., None]
    for sweep_index in range(SWEEPS):
        lse = sweep(
            flat_slots, pair_counts, source_rows, slot_coords, slot_potential - quarter_ny, slot_potential
        )
        if gather_all:
            came = lax.all_to_all(lse, "blocks", split_axis=0, concat_axis=0, tiled=True).reshape(peers, peers, cap, bs)
            mine = lax.dynamic_index_in_dim(came, me, axis=1, keepdims=False)
            potential_here = combine(mine[None], owned, potential_here, (1, 2))
            by_owner = jnp.transpose(came, (1, 0, 2, 3))[:, None]
            slot_potential = combine(
                by_owner, fetched, slot_potential.reshape(peers, cap, bs), (2, 3)
            ).reshape(nslot, 1, bs)
        else:
            came = lax.all_to_all(
                lse.reshape(peers, cap, bs), "blocks", split_axis=0, concat_axis=0, tiled=True
            )
            potential_here = combine(came[None], owned, potential_here, (1, 2))
            send_potential = potential_here[asked_local].reshape(peers, cap, bs)
            slot_potential = lax.all_to_all(
                send_potential, "blocks", split_axis=0, concat_axis=0, tiled=True
            ).reshape(nslot, 1, bs)

    source_side, drift = final(
        flat_slots, pair_counts, source_rows, source_coords, slot_coords, slot_rows, slot_potential - quarter_ny
    )
    return (source_side.reshape(-1), potential_here.reshape(-1), drift)


def solution(mesh):
    return jax.shard_map(
        local,
        mesh=mesh,
        in_specs=(
            P(None, ("groups", "blocks")),
            P(None, ("groups", "blocks")),
            P(("groups", "blocks")),
            P(("groups", "blocks"), None, None),
            P(("groups", "blocks"), None),
            P(("groups", "blocks")),
        ),
        out_specs=(P(("groups", "blocks")), P(("groups", "blocks")), P(None, ("groups", "blocks"))),
        check_vma=False,
    )
```

```python
import functools
import math

import jax
import jax.numpy as jnp
from jax import lax
from jax.experimental import pallas as pl
from jax.experimental.pallas import tpu as pltpu
from jax.sharding import PartitionSpec as P

SWEEPS = 2

floor_value = -1e30
PADDED = 32
CHUNK = 16
TAIL = 8
LOG2E = 1.4426950408889634
LN2 = 0.6931471805599453


def _pair_loop(cnt, body, carry):
    full = cnt // CHUNK
    carry = lax.fori_loop(0, full, lambda q, c: body(q * CHUNK, CHUNK, c), carry)
    rest = (cnt - full * CHUNK + TAIL - 1) // TAIL
    return lax.fori_loop(0, rest, lambda q, c: body(full * CHUNK + q * TAIL, TAIL, c), carry)


def _slots_at(slots_ref, s, p0, size, most):
    return [slots_ref[s * most + p0 + t] for t in range(size)]


def _rows_of(values):
    return jnp.concatenate(values, axis=0)


def _row_scores(s, cnt, slots_ref, xs, y_ref, h_ref, s_ref, most, bs):
    def first(p0, size, m):
        for t, sl in enumerate(_slots_at(slots_ref, s, p0, size, most)):
            hrow = jnp.where(p0 + t < cnt, h_ref[sl], floor_value)
            tile = (jnp.dot(xs, y_ref[sl], preferred_element_type=jnp.float32) + hrow) * LOG2E
            s_ref[p0 + t] = tile
            m = jnp.maximum(m, tile)
        return m

    m = _pair_loop(cnt, first, jnp.full((bs, bs), floor_value, jnp.float32))
    return jnp.max(m, axis=1, keepdims=True)


def sweep_kernel(slots_ref, counts_ref, xT_ref, y_ref, h_ref, g_ref, lse_ref, amax_ref, asum_ref, s_ref, *, most, log_mass):
    nblk, bs = xT_ref.shape[0], xT_ref.shape[1]
    amax_ref[...] = jnp.full(amax_ref.shape, floor_value, jnp.float32)
    asum_ref[...] = jnp.zeros(asum_ref.shape, jnp.float32)

    def block(s, carry):
        cnt = counts_ref[s]
        mrow = _row_scores(s, cnt, slots_ref, xT_ref[s], y_ref, h_ref, s_ref, most, bs)
        mb = jnp.broadcast_to(mrow, (bs, bs))

        def second(p0, size, acc):
            for t in range(size):
                acc = acc + jnp.exp2(s_ref[p0 + t] - mb)
            return acc

        acc = _pair_loop(cnt, second, jnp.zeros((bs, bs), jnp.float32))
        tot = jnp.sum(acc, axis=1, keepdims=True)
        kb = jnp.broadcast_to((log_mass - (mrow * LN2 + jnp.log(tot))) * LOG2E, (bs, bs))

        def column(p0, size, c):
            sls = _slots_at(slots_ref, s, p0, size, most)
            cms, ces = [], []
            for t in range(size):
                v = s_ref[p0 + t] + kb
                cm = jnp.max(v, axis=0, keepdims=True)
                cms.append(cm)
                ces.append(jnp.sum(jnp.exp2(v - cm), axis=0, keepdims=True))
            valid = lax.broadcasted_iota(jnp.int32, (size, bs), 0) + p0 < cnt
            tm = jnp.where(valid, _rows_of(cms) * LN2 - _rows_of([g_ref[sl] for sl in sls]), floor_value)
            te = jnp.where(valid, _rows_of(ces), 0.0)
            om = _rows_of([amax_ref[sl] for sl in sls])
            os = _rows_of([asum_ref[sl] for sl in sls])
            nm = jnp.maximum(om, tm)
            ns = os * jnp.exp(om - nm) + te * jnp.exp(tm - nm)
            for t, sl in enumerate(sls):
                amax_ref[sl] = nm[t : t + 1]
                asum_ref[sl] = ns[t : t + 1]
            return c

        _pair_loop(cnt, column, 0)
        return carry

    lax.fori_loop(0, nblk, block, 0)

    am = amax_ref[...]
    lse = jnp.where(am > 0.5 * floor_value, am + jnp.log(asum_ref[...]), floor_value)
    for d in range(lse_ref.shape[0]):
        lse_ref[d] = lse


def final_kernel(slots_ref, counts_ref, xT_ref, x_ref, y_ref, yT_ref, h_ref, f_ref, drift_ref, s_ref, *, most, log_mass, ncomp):
    nblk, bs = xT_ref.shape[0], xT_ref.shape[1]
    lanes = lax.broadcasted_iota(jnp.int32, (bs, yT_ref.shape[2]), 1)

    def block(s, carry):
        cnt = counts_ref[s]
        xs = xT_ref[s]
        mrow = _row_scores(s, cnt, slots_ref, xs, y_ref, h_ref, s_ref, most, bs)
        mb = jnp.broadcast_to(mrow, (bs, bs))

        def second(p0, size, c):
            acc, num = c
            for t, sl in enumerate(_slots_at(slots_ref, s, p0, size, most)):
                e = jnp.exp2(s_ref[p0 + t] - mb)
                acc = acc + e
                num = num + jnp.dot(e.astype(jnp.bfloat16), yT_ref[sl], preferred_element_type=jnp.float32)
            return acc, num

        acc, num = _pair_loop(
            cnt, second, (jnp.zeros((bs, bs), jnp.float32), jnp.zeros((bs, yT_ref.shape[2]), jnp.float32))
        )
        tot = jnp.sum(acc, axis=1, keepdims=True)
        xf = xs.astype(jnp.float32)
        quarter_nx = jnp.sum(xf * xf, axis=1, keepdims=True)
        fcol = log_mass - (mrow * LN2 + jnp.log(tot)) + quarter_nx
        packed = jnp.where(lanes == PADDED - 1, jnp.broadcast_to(fcol, num.shape), num)
        rows = jnp.transpose(packed)
        f_ref[s] = rows[PADDED - 1 : PADDED, :]
        off = pl.multiple_of(s * bs, bs)
        xcols = x_ref[:, pl.ds(off, bs)].astype(jnp.float32)
        drift_ref[:, pl.ds(off, bs)] = rows[:ncomp] / rows[ncomp : ncomp + 1] - xcols
        return carry

    lax.fori_loop(0, nblk, block, 0)


def _specs(kinds):
    return [pl.BlockSpec(memory_space=pltpu.SMEM if k == "s" else pltpu.VMEM) for k in kinds]


def local(source_coords, target_coords, target_potential, fetch_blocks, pair_slots, pair_counts):
    ncomp = source_coords.shape[0]
    nblk = pair_counts.shape[0]
    bs = source_coords.shape[1] // nblk
    peers = lax.axis_size("blocks")
    cap = fetch_blocks.shape[2]
    nslot = peers * cap
    most = pair_slots.shape[1]
    log_mass = -math.log(peers * nblk * bs)
    assert most % TAIL == 0

    wanted = fetch_blocks[0]
    me = lax.axis_index("blocks")
    fetch_all = lax.all_to_all(
        jnp.broadcast_to(wanted[None], (peers, peers, cap)), "blocks", split_axis=0, concat_axis=0, tiled=True
    )
    asked = lax.dynamic_index_in_dim(fetch_all, me, axis=1, keepdims=False)
    asked_local = (asked % nblk).reshape(-1)

    potential_here = target_potential.reshape(nblk, bs)
    high_wide = lax.reduce_precision(potential_here, exponent_bits=8, mantissa_bits=7)
    rest = potential_here - high_wide
    middle_wide = lax.reduce_precision(rest, exponent_bits=8, mantissa_bits=7)
    high = high_wide.astype(jnp.bfloat16)
    middle = middle_wide.astype(jnp.bfloat16)
    low = (rest - middle_wide).astype(jnp.bfloat16)
    target_blocks = jnp.concatenate(
        [jnp.transpose(target_coords.reshape(ncomp, nblk, bs), (1, 0, 2)), high[:, None], middle[:, None], low[:, None]],
        axis=1,
    )
    send = target_blocks[asked_local].reshape(peers, cap, ncomp + 3, bs)
    came = lax.all_to_all(send, "blocks", split_axis=0, concat_axis=0, tiled=True).reshape(nslot, ncomp + 3, bs)
    pieces = came[:, ncomp:, :].astype(jnp.float32)
    slot_potential = (pieces[:, 0:1] + pieces[:, 1:2]) + pieces[:, 2:3]
    came_coords = came[:, :ncomp, :]
    came_wide = came_coords.astype(jnp.float32)
    quarter_ny = 0.25 * jnp.sum(came_wide * came_wide, axis=1, keepdims=True)
    slot_coords = jnp.concatenate(
        [
            came_coords,
            jnp.ones((nslot, 1, bs), jnp.bfloat16),
            jnp.zeros((nslot, PADDED - ncomp - 1, bs), jnp.bfloat16),
        ],
        axis=1,
    )
    slot_rows = jnp.concatenate(
        [jnp.transpose(slot_coords, (0, 2, 1)), jnp.zeros((nslot, bs, bs - PADDED), jnp.bfloat16)], axis=2
    )
    halved = (source_coords.astype(jnp.float32) * 0.5).astype(jnp.bfloat16)
    halved = jnp.concatenate([halved, jnp.zeros((PADDED - ncomp, nblk * bs), jnp.bfloat16)], axis=0)
    source_rows = jnp.transpose(halved.reshape(PADDED, nblk, bs), (1, 2, 0))
    flat_slots = pair_slots.reshape(-1)

    vmem = 48 * 1024 * 1024
    scratch = [pltpu.VMEM((nslot, 1, bs), jnp.float32), pltpu.VMEM((most, bs, bs), jnp.float32)]
    gather_all = peers * nslot * bs * 4 <= (1 << 20)
    copies = peers if gather_all else 1
    sweep = pl.pallas_call(
        functools.partial(sweep_kernel, most=most, log_mass=log_mass),
        out_shape=jax.ShapeDtypeStruct((copies, nslot, 1, bs), jnp.float32),
        in_specs=_specs("ssvvvv"),
        out_specs=_specs("v")[0],
        scratch_shapes=[pltpu.VMEM((nslot, 1, bs), jnp.float32)] * 2 + scratch[1:],
        compiler_params=pltpu.CompilerParams(vmem_limit_bytes=vmem),
    )
    final = pl.pallas_call(
        functools.partial(final_kernel, most=most, log_mass=log_mass, ncomp=ncomp),
        out_shape=(
            jax.ShapeDtypeStruct((nblk, 1, bs), jnp.float32),
            jax.ShapeDtypeStruct((ncomp, nblk * bs), jnp.float32),
        ),
        in_specs=_specs("ssvvvvv"),
        out_specs=tuple(_specs("vv")),
        scratch_shapes=scratch[1:],
        compiler_params=pltpu.CompilerParams(vmem_limit_bytes=vmem),
    )

    def combine(values, match, previous, axes):
        merged = jnp.max(jnp.where(match, values, floor_value), axis=axes)
        summed = jnp.sum(jnp.where(match, jnp.exp(values - jnp.expand_dims(merged, axes)), 0.0), axis=axes)
        reached = merged > 0.5 * floor_value
        return jnp.where(reached, log_mass - (merged + jnp.log(jnp.where(reached, summed, 1.0))), previous)

    owned = (asked_local.reshape(peers, cap)[None] == jnp.arange(nblk, dtype=jnp.int32)[:, None, None])[..., None]
    if gather_all:
        fetched = jnp.transpose(fetch_all, (1, 0, 2))[:, None, :, :] == wanted[:, :, None, None]
        fetched = fetched[..., None]
    for sweep_index in range(SWEEPS):
        lse = sweep(
            flat_slots, pair_counts, source_rows, slot_coords, slot_potential - quarter_ny, slot_potential
        )
        if gather_all:
            came = lax.all_to_all(lse, "blocks", split_axis=0, concat_axis=0, tiled=True).reshape(peers, peers, cap, bs)
            mine = lax.dynamic_index_in_dim(came, me, axis=1, keepdims=False)
            potential_here = combine(mine[None], owned, potential_here, (1, 2))
            by_owner = jnp.transpose(came, (1, 0, 2, 3))[:, None]
            slot_potential = combine(
                by_owner, fetched, slot_potential.reshape(peers, cap, bs), (2, 3)
            ).reshape(nslot, 1, bs)
        else:
            came = lax.all_to_all(
                lse.reshape(peers, cap, bs), "blocks", split_axis=0, concat_axis=0, tiled=True
            )
            potential_here = combine(came[None], owned, potential_here, (1, 2))
            send_potential = potential_here[asked_local].reshape(peers, cap, bs)
            slot_potential = lax.all_to_all(
                send_potential, "blocks", split_axis=0, concat_axis=0, tiled=True
            ).reshape(nslot, 1, bs)

    source_side, drift = final(
        flat_slots, pair_counts, source_rows, source_coords, slot_coords, slot_rows, slot_potential - quarter_ny
    )
    return (source_side.reshape(-1), potential_here.reshape(-1), drift)


def solution(mesh):
    return jax.shard_map(
        local,
        mesh=mesh,
        in_specs=(
            P(None, ("groups", "blocks")),
            P(None, ("groups", "blocks")),
            P(("groups", "blocks")),
            P(("groups", "blocks"), None, None),
            P(("groups", "blocks"), None),
            P(("groups", "blocks")),
        ),
        out_specs=(P(("groups", "blocks")), P(("groups", "blocks")), P(None, ("groups", "blocks"))),
        check_vma=False,
    )
```

```python
import functools
import math

import jax
import jax.numpy as jnp
from jax import lax
from jax.experimental import pallas as pl
from jax.experimental.pallas import tpu as pltpu
from jax.sharding import PartitionSpec as P

SWEEPS = 2

floor_value = -1e30
PADDED = 32
CHUNK = 32
TAIL = 16
LOG2E = 1.4426950408889634
LN2 = 0.6931471805599453


def _pair_loop(cnt, body, carry):
    full = cnt // CHUNK
    carry = lax.fori_loop(0, full, lambda q, c: body(q * CHUNK, CHUNK, c), carry)
    rest = (cnt - full * CHUNK + TAIL - 1) // TAIL
    return lax.fori_loop(0, rest, lambda q, c: body(full * CHUNK + q * TAIL, TAIL, c), carry)


def _slots_at(slots_ref, s, p0, size, most):
    return [slots_ref[s * most + p0 + t] for t in range(size)]


def _rows_of(values):
    return jnp.concatenate(values, axis=0)


def _row_scores(s, cnt, slots_ref, xs, y_ref, h_ref, s_ref, most, bs):
    def first(p0, size, m):
        for t, sl in enumerate(_slots_at(slots_ref, s, p0, size, most)):
            hrow = jnp.where(p0 + t < cnt, h_ref[sl], floor_value)
            tile = (jnp.dot(xs, y_ref[sl], preferred_element_type=jnp.float32) + hrow) * LOG2E
            s_ref[p0 + t] = tile
            m = jnp.maximum(m, tile)
        return m

    m = _pair_loop(cnt, first, jnp.full((bs, bs), floor_value, jnp.float32))
    return jnp.max(m, axis=1, keepdims=True)


def sweep_kernel(slots_ref, counts_ref, xT_ref, y_ref, h_ref, g_ref, lse_ref, amax_ref, asum_ref, s_ref, *, most, log_mass):
    nblk, bs = xT_ref.shape[0], xT_ref.shape[1]
    amax_ref[...] = jnp.full(amax_ref.shape, floor_value, jnp.float32)
    asum_ref[...] = jnp.zeros(asum_ref.shape, jnp.float32)

    def block(s, carry):
        cnt = counts_ref[s]
        mrow = _row_scores(s, cnt, slots_ref, xT_ref[s], y_ref, h_ref, s_ref, most, bs)
        mb = jnp.broadcast_to(mrow, (bs, bs))

        def second(p0, size, acc):
            for t in range(size):
                acc = acc + jnp.exp2(s_ref[p0 + t] - mb)
            return acc

        acc = _pair_loop(cnt, second, jnp.zeros((bs, bs), jnp.float32))
        tot = jnp.sum(acc, axis=1, keepdims=True)
        kb = jnp.broadcast_to((log_mass - (mrow * LN2 + jnp.log(tot))) * LOG2E, (bs, bs))

        def column(p0, size, c):
            sls = _slots_at(slots_ref, s, p0, size, most)
            cms, ces = [], []
            for t in range(size):
                v = s_ref[p0 + t] + kb
                cm = jnp.max(v, axis=0, keepdims=True)
                cms.append(cm)
                ces.append(jnp.sum(jnp.exp2(v - cm), axis=0, keepdims=True))
            valid = lax.broadcasted_iota(jnp.int32, (size, bs), 0) + p0 < cnt
            tm = jnp.where(valid, _rows_of(cms) * LN2 - _rows_of([g_ref[sl] for sl in sls]), floor_value)
            te = jnp.where(valid, _rows_of(ces), 0.0)
            om = _rows_of([amax_ref[sl] for sl in sls])
            os = _rows_of([asum_ref[sl] for sl in sls])
            nm = jnp.maximum(om, tm)
            ns = os * jnp.exp(om - nm) + te * jnp.exp(tm - nm)
            for t, sl in enumerate(sls):
                amax_ref[sl] = nm[t : t + 1]
                asum_ref[sl] = ns[t : t + 1]
            return c

        _pair_loop(cnt, column, 0)
        return carry

    lax.fori_loop(0, nblk, block, 0)

    am = amax_ref[...]
    lse = jnp.where(am > 0.5 * floor_value, am + jnp.log(asum_ref[...]), floor_value)
    for d in range(lse_ref.shape[0]):
        lse_ref[d] = lse


def final_kernel(slots_ref, counts_ref, xT_ref, x_ref, y_ref, yT_ref, h_ref, f_ref, drift_ref, s_ref, *, most, log_mass, ncomp):
    nblk, bs = xT_ref.shape[0], xT_ref.shape[1]
    lanes = lax.broadcasted_iota(jnp.int32, (bs, yT_ref.shape[2]), 1)

    def block(s, carry):
        cnt = counts_ref[s]
        xs = xT_ref[s]
        mrow = _row_scores(s, cnt, slots_ref, xs, y_ref, h_ref, s_ref, most, bs)
        mb = jnp.broadcast_to(mrow, (bs, bs))

        def second(p0, size, c):
            acc, num = c
            for t, sl in enumerate(_slots_at(slots_ref, s, p0, size, most)):
                e = jnp.exp2(s_ref[p0 + t] - mb)
                acc = acc + e
                num = num + jnp.dot(e.astype(jnp.bfloat16), yT_ref[sl], preferred_element_type=jnp.float32)
            return acc, num

        acc, num = _pair_loop(
            cnt, second, (jnp.zeros((bs, bs), jnp.float32), jnp.zeros((bs, yT_ref.shape[2]), jnp.float32))
        )
        tot = jnp.sum(acc, axis=1, keepdims=True)
        xf = xs.astype(jnp.float32)
        quarter_nx = jnp.sum(xf * xf, axis=1, keepdims=True)
        fcol = log_mass - (mrow * LN2 + jnp.log(tot)) + quarter_nx
        packed = jnp.where(lanes == PADDED - 1, jnp.broadcast_to(fcol, num.shape), num)
        rows = jnp.transpose(packed)
        f_ref[s] = rows[PADDED - 1 : PADDED, :]
        off = pl.multiple_of(s * bs, bs)
        xcols = x_ref[:, pl.ds(off, bs)].astype(jnp.float32)
        drift_ref[:, pl.ds(off, bs)] = rows[:ncomp] / rows[ncomp : ncomp + 1] - xcols
        return carry

    lax.fori_loop(0, nblk, block, 0)


def _specs(kinds):
    return [pl.BlockSpec(memory_space=pltpu.SMEM if k == "s" else pltpu.VMEM) for k in kinds]


def local(source_coords, target_coords, target_potential, fetch_blocks, pair_slots, pair_counts):
    ncomp = source_coords.shape[0]
    nblk = pair_counts.shape[0]
    bs = source_coords.shape[1] // nblk
    peers = lax.axis_size("blocks")
    cap = fetch_blocks.shape[2]
    nslot = peers * cap
    most = pair_slots.shape[1]
    log_mass = -math.log(peers * nblk * bs)
    assert most % TAIL == 0

    wanted = fetch_blocks[0]
    me = lax.axis_index("blocks")
    fetch_all = lax.all_to_all(
        jnp.broadcast_to(wanted[None], (peers, peers, cap)), "blocks", split_axis=0, concat_axis=0, tiled=True
    )
    asked = lax.dynamic_index_in_dim(fetch_all, me, axis=1, keepdims=False)
    asked_local = (asked % nblk).reshape(-1)

    potential_here = target_potential.reshape(nblk, bs)
    high_wide = lax.reduce_precision(potential_here, exponent_bits=8, mantissa_bits=7)
    rest = potential_here - high_wide
    middle_wide = lax.reduce_precision(rest, exponent_bits=8, mantissa_bits=7)
    high = high_wide.astype(jnp.bfloat16)
    middle = middle_wide.astype(jnp.bfloat16)
    low = (rest - middle_wide).astype(jnp.bfloat16)
    target_blocks = jnp.concatenate(
        [jnp.transpose(target_coords.reshape(ncomp, nblk, bs), (1, 0, 2)), high[:, None], middle[:, None], low[:, None]],
        axis=1,
    )
    send = target_blocks[asked_local].reshape(peers, cap, ncomp + 3, bs)
    came = lax.all_to_all(send, "blocks", split_axis=0, concat_axis=0, tiled=True).reshape(nslot, ncomp + 3, bs)
    pieces = came[:, ncomp:, :].astype(jnp.float32)
    slot_potential = (pieces[:, 0:1] + pieces[:, 1:2]) + pieces[:, 2:3]
    came_coords = came[:, :ncomp, :]
    came_wide = came_coords.astype(jnp.float32)
    quarter_ny = 0.25 * jnp.sum(came_wide * came_wide, axis=1, keepdims=True)
    slot_coords = jnp.concatenate(
        [
            came_coords,
            jnp.ones((nslot, 1, bs), jnp.bfloat16),
            jnp.zeros((nslot, PADDED - ncomp - 1, bs), jnp.bfloat16),
        ],
        axis=1,
    )
    slot_rows = jnp.concatenate(
        [jnp.transpose(slot_coords, (0, 2, 1)), jnp.zeros((nslot, bs, bs - PADDED), jnp.bfloat16)], axis=2
    )
    halved = (source_coords.astype(jnp.float32) * 0.5).astype(jnp.bfloat16)
    halved = jnp.concatenate([halved, jnp.zeros((PADDED - ncomp, nblk * bs), jnp.bfloat16)], axis=0)
    source_rows = jnp.transpose(halved.reshape(PADDED, nblk, bs), (1, 2, 0))
    flat_slots = pair_slots.reshape(-1)

    vmem = 48 * 1024 * 1024
    scratch = [pltpu.VMEM((nslot, 1, bs), jnp.float32), pltpu.VMEM((most, bs, bs), jnp.float32)]
    gather_all = peers * nslot * bs * 4 <= (1 << 20)
    copies = peers if gather_all else 1
    sweep = pl.pallas_call(
        functools.partial(sweep_kernel, most=most, log_mass=log_mass),
        out_shape=jax.ShapeDtypeStruct((copies, nslot, 1, bs), jnp.float32),
        in_specs=_specs("ssvvvv"),
        out_specs=_specs("v")[0],
        scratch_shapes=[pltpu.VMEM((nslot, 1, bs), jnp.float32)] * 2 + scratch[1:],
        compiler_params=pltpu.CompilerParams(vmem_limit_bytes=vmem),
    )
    final = pl.pallas_call(
        functools.partial(final_kernel, most=most, log_mass=log_mass, ncomp=ncomp),
        out_shape=(
            jax.ShapeDtypeStruct((nblk, 1, bs), jnp.float32),
            jax.ShapeDtypeStruct((ncomp, nblk * bs), jnp.float32),
        ),
        in_specs=_specs("ssvvvvv"),
        out_specs=tuple(_specs("vv")),
        scratch_shapes=scratch[1:],
        compiler_params=pltpu.CompilerParams(vmem_limit_bytes=vmem),
    )

    def combine(values, match, previous, axes):
        merged = jnp.max(jnp.where(match, values, floor_value), axis=axes)
        summed = jnp.sum(jnp.where(match, jnp.exp(values - jnp.expand_dims(merged, axes)), 0.0), axis=axes)
        reached = merged > 0.5 * floor_value
        return jnp.where(reached, log_mass - (merged + jnp.log(jnp.where(reached, summed, 1.0))), previous)

    owned = (asked_local.reshape(peers, cap)[None] == jnp.arange(nblk, dtype=jnp.int32)[:, None, None])[..., None]
    if gather_all:
        fetched = jnp.transpose(fetch_all, (1, 0, 2))[:, None, :, :] == wanted[:, :, None, None]
        fetched = fetched[..., None]
    for sweep_index in range(SWEEPS):
        lse = sweep(
            flat_slots, pair_counts, source_rows, slot_coords, slot_potential - quarter_ny, slot_potential
        )
        if gather_all:
            came = lax.all_to_all(lse, "blocks", split_axis=0, concat_axis=0, tiled=True).reshape(peers, peers, cap, bs)
            mine = lax.dynamic_index_in_dim(came, me, axis=1, keepdims=False)
            potential_here = combine(mine[None], owned, potential_here, (1, 2))
            by_owner = jnp.transpose(came, (1, 0, 2, 3))[:, None]
            slot_potential = combine(
                by_owner, fetched, slot_potential.reshape(peers, cap, bs), (2, 3)
            ).reshape(nslot, 1, bs)
        else:
            came = lax.all_to_all(
                lse.reshape(peers, cap, bs), "blocks", split_axis=0, concat_axis=0, tiled=True
            )
            potential_here = combine(came[None], owned, potential_here, (1, 2))
            send_potential = potential_here[asked_local].reshape(peers, cap, bs)
            slot_potential = lax.all_to_all(
                send_potential, "blocks", split_axis=0, concat_axis=0, tiled=True
            ).reshape(nslot, 1, bs)

    source_side, drift = final(
        flat_slots, pair_counts, source_rows, source_coords, slot_coords, slot_rows, slot_potential - quarter_ny
    )
    return (source_side.reshape(-1), potential_here.reshape(-1), drift)


def solution(mesh):
    return jax.shard_map(
        local,
        mesh=mesh,
        in_specs=(
            P(None, ("groups", "blocks")),
            P(None, ("groups", "blocks")),
            P(("groups", "blocks")),
            P(("groups", "blocks"), None, None),
            P(("groups", "blocks"), None),
            P(("groups", "blocks")),
        ),
        out_specs=(P(("groups", "blocks")), P(("groups", "blocks")), P(None, ("groups", "blocks"))),
        check_vma=False,
    )
```

```python
import functools
import math

import jax
import jax.numpy as jnp
from jax import lax
from jax.experimental import pallas as pl
from jax.experimental.pallas import tpu as pltpu
from jax.sharding import PartitionSpec as P

SWEEPS = 2

floor_value = -1e30
PADDED = 32
CHUNK = 32
TAIL = 32
LOG2E = 1.4426950408889634
LN2 = 0.6931471805599453


def _pair_loop(cnt, body, carry):
    full = cnt // CHUNK
    carry = lax.fori_loop(0, full, lambda q, c: body(q * CHUNK, CHUNK, c), carry)
    rest = (cnt - full * CHUNK + TAIL - 1) // TAIL
    return lax.fori_loop(0, rest, lambda q, c: body(full * CHUNK + q * TAIL, TAIL, c), carry)


def _slots_at(slots_ref, s, p0, size, most):
    return [slots_ref[s * most + p0 + t] for t in range(size)]


def _rows_of(values):
    return jnp.concatenate(values, axis=0)


def _row_scores(s, cnt, slots_ref, xs, y_ref, h_ref, s_ref, most, bs):
    def first(p0, size, m):
        for t, sl in enumerate(_slots_at(slots_ref, s, p0, size, most)):
            hrow = jnp.where(p0 + t < cnt, h_ref[sl], floor_value)
            tile = (jnp.dot(xs, y_ref[sl], preferred_element_type=jnp.float32) + hrow) * LOG2E
            s_ref[p0 + t] = tile
            m = jnp.maximum(m, tile)
        return m

    m = _pair_loop(cnt, first, jnp.full((bs, bs), floor_value, jnp.float32))
    return jnp.max(m, axis=1, keepdims=True)


def sweep_kernel(slots_ref, counts_ref, xT_ref, y_ref, h_ref, g_ref, lse_ref, amax_ref, asum_ref, s_ref, *, most, log_mass):
    nblk, bs = xT_ref.shape[0], xT_ref.shape[1]
    amax_ref[...] = jnp.full(amax_ref.shape, floor_value, jnp.float32)
    asum_ref[...] = jnp.zeros(asum_ref.shape, jnp.float32)

    def block(s, carry):
        cnt = counts_ref[s]
        mrow = _row_scores(s, cnt, slots_ref, xT_ref[s], y_ref, h_ref, s_ref, most, bs)
        mb = jnp.broadcast_to(mrow, (bs, bs))

        def second(p0, size, acc):
            for t in range(size):
                acc = acc + jnp.exp2(s_ref[p0 + t] - mb)
            return acc

        acc = _pair_loop(cnt, second, jnp.zeros((bs, bs), jnp.float32))
        tot = jnp.sum(acc, axis=1, keepdims=True)
        kb = jnp.broadcast_to((log_mass - (mrow * LN2 + jnp.log(tot))) * LOG2E, (bs, bs))

        def column(p0, size, c):
            sls = _slots_at(slots_ref, s, p0, size, most)
            cms, ces = [], []
            for t in range(size):
                v = s_ref[p0 + t] + kb
                cm = jnp.max(v, axis=0, keepdims=True)
                cms.append(cm)
                ces.append(jnp.sum(jnp.exp2(v - cm), axis=0, keepdims=True))
            valid = lax.broadcasted_iota(jnp.int32, (size, bs), 0) + p0 < cnt
            tm = jnp.where(valid, _rows_of(cms) * LN2 - _rows_of([g_ref[sl] for sl in sls]), floor_value)
            te = jnp.where(valid, _rows_of(ces), 0.0)
            om = _rows_of([amax_ref[sl] for sl in sls])
            os = _rows_of([asum_ref[sl] for sl in sls])
            nm = jnp.maximum(om, tm)
            ns = os * jnp.exp(om - nm) + te * jnp.exp(tm - nm)
            for t, sl in enumerate(sls):
                amax_ref[sl] = nm[t : t + 1]
                asum_ref[sl] = ns[t : t + 1]
            return c

        _pair_loop(cnt, column, 0)
        return carry

    lax.fori_loop(0, nblk, block, 0)

    am = amax_ref[...]
    lse = jnp.where(am > 0.5 * floor_value, am + jnp.log(asum_ref[...]), floor_value)
    for d in range(lse_ref.shape[0]):
        lse_ref[d] = lse


def final_kernel(slots_ref, counts_ref, xT_ref, x_ref, y_ref, yT_ref, h_ref, f_ref, drift_ref, s_ref, *, most, log_mass, ncomp):
    nblk, bs = xT_ref.shape[0], xT_ref.shape[1]
    lanes = lax.broadcasted_iota(jnp.int32, (bs, yT_ref.shape[2]), 1)

    def block(s, carry):
        cnt = counts_ref[s]
        xs = xT_ref[s]
        mrow = _row_scores(s, cnt, slots_ref, xs, y_ref, h_ref, s_ref, most, bs)
        mb = jnp.broadcast_to(mrow, (bs, bs))

        def second(p0, size, c):
            acc, num = c
            for t, sl in enumerate(_slots_at(slots_ref, s, p0, size, most)):
                e = jnp.exp2(s_ref[p0 + t] - mb)
                acc = acc + e
                num = num + jnp.dot(e.astype(jnp.bfloat16), yT_ref[sl], preferred_element_type=jnp.float32)
            return acc, num

        acc, num = _pair_loop(
            cnt, second, (jnp.zeros((bs, bs), jnp.float32), jnp.zeros((bs, yT_ref.shape[2]), jnp.float32))
        )
        tot = jnp.sum(acc, axis=1, keepdims=True)
        xf = xs.astype(jnp.float32)
        quarter_nx = jnp.sum(xf * xf, axis=1, keepdims=True)
        fcol = log_mass - (mrow * LN2 + jnp.log(tot)) + quarter_nx
        packed = jnp.where(lanes == PADDED - 1, jnp.broadcast_to(fcol, num.shape), num)
        rows = jnp.transpose(packed)
        f_ref[s] = rows[PADDED - 1 : PADDED, :]
        off = pl.multiple_of(s * bs, bs)
        xcols = x_ref[:, pl.ds(off, bs)].astype(jnp.float32)
        drift_ref[:, pl.ds(off, bs)] = rows[:ncomp] / rows[ncomp : ncomp + 1] - xcols
        return carry

    lax.fori_loop(0, nblk, block, 0)


def _specs(kinds):
    return [pl.BlockSpec(memory_space=pltpu.SMEM if k == "s" else pltpu.VMEM) for k in kinds]


def local(source_coords, target_coords, target_potential, fetch_blocks, pair_slots, pair_counts):
    ncomp = source_coords.shape[0]
    nblk = pair_counts.shape[0]
    bs = source_coords.shape[1] // nblk
    peers = lax.axis_size("blocks")
    cap = fetch_blocks.shape[2]
    nslot = peers * cap
    most = pair_slots.shape[1]
    log_mass = -math.log(peers * nblk * bs)
    assert most % TAIL == 0

    wanted = fetch_blocks[0]
    me = lax.axis_index("blocks")
    fetch_all = lax.all_to_all(
        jnp.broadcast_to(wanted[None], (peers, peers, cap)), "blocks", split_axis=0, concat_axis=0, tiled=True
    )
    asked = lax.dynamic_index_in_dim(fetch_all, me, axis=1, keepdims=False)
    asked_local = (asked % nblk).reshape(-1)

    potential_here = target_potential.reshape(nblk, bs)
    high_wide = lax.reduce_precision(potential_here, exponent_bits=8, mantissa_bits=7)
    rest = potential_here - high_wide
    middle_wide = lax.reduce_precision(rest, exponent_bits=8, mantissa_bits=7)
    high = high_wide.astype(jnp.bfloat16)
    middle = middle_wide.astype(jnp.bfloat16)
    low = (rest - middle_wide).astype(jnp.bfloat16)
    target_blocks = jnp.concatenate(
        [jnp.transpose(target_coords.reshape(ncomp, nblk, bs), (1, 0, 2)), high[:, None], middle[:, None], low[:, None]],
        axis=1,
    )
    send = target_blocks[asked_local].reshape(peers, cap, ncomp + 3, bs)
    came = lax.all_to_all(send, "blocks", split_axis=0, concat_axis=0, tiled=True).reshape(nslot, ncomp + 3, bs)
    pieces = came[:, ncomp:, :].astype(jnp.float32)
    slot_potential = (pieces[:, 0:1] + pieces[:, 1:2]) + pieces[:, 2:3]
    came_coords = came[:, :ncomp, :]
    came_wide = came_coords.astype(jnp.float32)
    quarter_ny = 0.25 * jnp.sum(came_wide * came_wide, axis=1, keepdims=True)
    slot_coords = jnp.concatenate(
        [
            came_coords,
            jnp.ones((nslot, 1, bs), jnp.bfloat16),
            jnp.zeros((nslot, PADDED - ncomp - 1, bs), jnp.bfloat16),
        ],
        axis=1,
    )
    slot_rows = jnp.concatenate(
        [jnp.transpose(slot_coords, (0, 2, 1)), jnp.zeros((nslot, bs, bs - PADDED), jnp.bfloat16)], axis=2
    )
    halved = (source_coords.astype(jnp.float32) * 0.5).astype(jnp.bfloat16)
    halved = jnp.concatenate([halved, jnp.zeros((PADDED - ncomp, nblk * bs), jnp.bfloat16)], axis=0)
    source_rows = jnp.transpose(halved.reshape(PADDED, nblk, bs), (1, 2, 0))
    flat_slots = pair_slots.reshape(-1)

    vmem = 48 * 1024 * 1024
    scratch = [pltpu.VMEM((nslot, 1, bs), jnp.float32), pltpu.VMEM((most, bs, bs), jnp.float32)]
    gather_all = peers * nslot * bs * 4 <= (1 << 20)
    copies = peers if gather_all else 1
    sweep = pl.pallas_call(
        functools.partial(sweep_kernel, most=most, log_mass=log_mass),
        out_shape=jax.ShapeDtypeStruct((copies, nslot, 1, bs), jnp.float32),
        in_specs=_specs("ssvvvv"),
        out_specs=_specs("v")[0],
        scratch_shapes=[pltpu.VMEM((nslot, 1, bs), jnp.float32)] * 2 + scratch[1:],
        compiler_params=pltpu.CompilerParams(vmem_limit_bytes=vmem),
    )
    final = pl.pallas_call(
        functools.partial(final_kernel, most=most, log_mass=log_mass, ncomp=ncomp),
        out_shape=(
            jax.ShapeDtypeStruct((nblk, 1, bs), jnp.float32),
            jax.ShapeDtypeStruct((ncomp, nblk * bs), jnp.float32),
        ),
        in_specs=_specs("ssvvvvv"),
        out_specs=tuple(_specs("vv")),
        scratch_shapes=scratch[1:],
        compiler_params=pltpu.CompilerParams(vmem_limit_bytes=vmem),
    )

    def combine(values, match, previous, axes):
        merged = jnp.max(jnp.where(match, values, floor_value), axis=axes)
        summed = jnp.sum(jnp.where(match, jnp.exp(values - jnp.expand_dims(merged, axes)), 0.0), axis=axes)
        reached = merged > 0.5 * floor_value
        return jnp.where(reached, log_mass - (merged + jnp.log(jnp.where(reached, summed, 1.0))), previous)

    owned = (asked_local.reshape(peers, cap)[None] == jnp.arange(nblk, dtype=jnp.int32)[:, None, None])[..., None]
    if gather_all:
        fetched = jnp.transpose(fetch_all, (1, 0, 2))[:, None, :, :] == wanted[:, :, None, None]
        fetched = fetched[..., None]
    for sweep_index in range(SWEEPS):
        lse = sweep(
            flat_slots, pair_counts, source_rows, slot_coords, slot_potential - quarter_ny, slot_potential
        )
        if gather_all:
            came = lax.all_to_all(lse, "blocks", split_axis=0, concat_axis=0, tiled=True).reshape(peers, peers, cap, bs)
            mine = lax.dynamic_index_in_dim(came, me, axis=1, keepdims=False)
            potential_here = combine(mine[None], owned, potential_here, (1, 2))
            by_owner = jnp.transpose(came, (1, 0, 2, 3))[:, None]
            slot_potential = combine(
                by_owner, fetched, slot_potential.reshape(peers, cap, bs), (2, 3)
            ).reshape(nslot, 1, bs)
        else:
            came = lax.all_to_all(
                lse.reshape(peers, cap, bs), "blocks", split_axis=0, concat_axis=0, tiled=True
            )
            potential_here = combine(came[None], owned, potential_here, (1, 2))
            send_potential = potential_here[asked_local].reshape(peers, cap, bs)
            slot_potential = lax.all_to_all(
                send_potential, "blocks", split_axis=0, concat_axis=0, tiled=True
            ).reshape(nslot, 1, bs)

    source_side, drift = final(
        flat_slots, pair_counts, source_rows, source_coords, slot_coords, slot_rows, slot_potential - quarter_ny
    )
    return (source_side.reshape(-1), potential_here.reshape(-1), drift)


def solution(mesh):
    return jax.shard_map(
        local,
        mesh=mesh,
        in_specs=(
            P(None, ("groups", "blocks")),
            P(None, ("groups", "blocks")),
            P(("groups", "blocks")),
            P(("groups", "blocks"), None, None),
            P(("groups", "blocks"), None),
            P(("groups", "blocks")),
        ),
        out_specs=(P(("groups", "blocks")), P(("groups", "blocks")), P(None, ("groups", "blocks"))),
        check_vma=False,
    )
```

```python
import functools
import math

import jax
import jax.numpy as jnp
from jax import lax
from jax.experimental import pallas as pl
from jax.experimental.pallas import tpu as pltpu
from jax.sharding import PartitionSpec as P

SWEEPS = 2

floor_value = -1e30
PADDED = 32
CHUNK = 16
TAIL = 16
LOG2E = 1.4426950408889634
LN2 = 0.6931471805599453


def _pair_loop(cnt, body, carry):
    full = cnt // CHUNK
    carry = lax.fori_loop(0, full, lambda q, c: body(q * CHUNK, CHUNK, c), carry)
    rest = (cnt - full * CHUNK + TAIL - 1) // TAIL
    return lax.fori_loop(0, rest, lambda q, c: body(full * CHUNK + q * TAIL, TAIL, c), carry)


def _slots_at(slots_ref, s, p0, size, most):
    return [slots_ref[s * most + p0 + t] for t in range(size)]


def _rows_of(values):
    return jnp.concatenate(values, axis=0)


def _row_scores(s, cnt, slots_ref, xs, y_ref, h_ref, s_ref, most, bs):
    def first(p0, size, m):
        for t, sl in enumerate(_slots_at(slots_ref, s, p0, size, most)):
            hrow = jnp.where(p0 + t < cnt, h_ref[sl], floor_value)
            tile = (jnp.dot(xs, y_ref[sl], preferred_element_type=jnp.float32) + hrow) * LOG2E
            s_ref[p0 + t] = tile
            m = jnp.maximum(m, tile)
        return m

    m = _pair_loop(cnt, first, jnp.full((bs, bs), floor_value, jnp.float32))
    return jnp.max(m, axis=1, keepdims=True)


def sweep_kernel(slots_ref, counts_ref, xT_ref, y_ref, h_ref, g_ref, lse_ref, amax_ref, asum_ref, s_ref, *, most, log_mass):
    nblk, bs = xT_ref.shape[0], xT_ref.shape[1]
    amax_ref[...] = jnp.full(amax_ref.shape, floor_value, jnp.float32)
    asum_ref[...] = jnp.zeros(asum_ref.shape, jnp.float32)

    def block(s, carry):
        cnt = counts_ref[s]
        mrow = _row_scores(s, cnt, slots_ref, xT_ref[s], y_ref, h_ref, s_ref, most, bs)
        mb = jnp.broadcast_to(mrow, (bs, bs))

        def second(p0, size, acc):
            for t in range(size):
                acc = acc + jnp.exp2(s_ref[p0 + t] - mb)
            return acc

        acc = _pair_loop(cnt, second, jnp.zeros((bs, bs), jnp.float32))
        tot = jnp.sum(acc, axis=1, keepdims=True)
        kb = jnp.broadcast_to((log_mass - (mrow * LN2 + jnp.log(tot))) * LOG2E, (bs, bs))

        def column(p0, size, c):
            sls = _slots_at(slots_ref, s, p0, size, most)
            cms, ces = [], []
            for t in range(size):
                v = s_ref[p0 + t] + kb
                cm = jnp.max(v, axis=0, keepdims=True)
                cms.append(cm)
                ces.append(jnp.sum(jnp.exp2(v - cm), axis=0, keepdims=True))
            valid = lax.broadcasted_iota(jnp.int32, (size, bs), 0) + p0 < cnt
            tm = jnp.where(valid, _rows_of(cms) * LN2 - _rows_of([g_ref[sl] for sl in sls]), floor_value)
            te = jnp.where(valid, _rows_of(ces), 0.0)
            om = _rows_of([amax_ref[sl] for sl in sls])
            os = _rows_of([asum_ref[sl] for sl in sls])
            nm = jnp.maximum(om, tm)
            ns = os * jnp.exp(om - nm) + te * jnp.exp(tm - nm)
            for t, sl in enumerate(sls):
                amax_ref[sl] = nm[t : t + 1]
                asum_ref[sl] = ns[t : t + 1]
            return c

        _pair_loop(cnt, column, 0)
        return carry

    lax.fori_loop(0, nblk, block, 0)

    am = amax_ref[...]
    lse = jnp.where(am > 0.5 * floor_value, am + jnp.log(asum_ref[...]), floor_value)
    for d in range(lse_ref.shape[0]):
        lse_ref[d] = lse


def final_kernel(slots_ref, counts_ref, xT_ref, x_ref, y_ref, yT_ref, h_ref, f_ref, drift_ref, s_ref, *, most, log_mass, ncomp):
    nblk, bs = xT_ref.shape[0], xT_ref.shape[1]
    lanes = lax.broadcasted_iota(jnp.int32, (bs, yT_ref.shape[2]), 1)

    def block(s, carry):
        cnt = counts_ref[s]
        xs = xT_ref[s]
        mrow = _row_scores(s, cnt, slots_ref, xs, y_ref, h_ref, s_ref, most, bs)
        mb = jnp.broadcast_to(mrow, (bs, bs))

        def second(p0, size, c):
            acc, num = c
            for t, sl in enumerate(_slots_at(slots_ref, s, p0, size, most)):
                e = jnp.exp2(s_ref[p0 + t] - mb)
                acc = acc + e
                num = num + jnp.dot(e.astype(jnp.bfloat16), yT_ref[sl], preferred_element_type=jnp.float32)
            return acc, num

        acc, num = _pair_loop(
            cnt, second, (jnp.zeros((bs, bs), jnp.float32), jnp.zeros((bs, yT_ref.shape[2]), jnp.float32))
        )
        tot = jnp.sum(acc, axis=1, keepdims=True)
        xf = xs.astype(jnp.float32)
        quarter_nx = jnp.sum(xf * xf, axis=1, keepdims=True)
        fcol = log_mass - (mrow * LN2 + jnp.log(tot)) + quarter_nx
        packed = jnp.where(lanes == PADDED - 1, jnp.broadcast_to(fcol, num.shape), num)
        rows = jnp.transpose(packed)
        f_ref[s] = rows[PADDED - 1 : PADDED, :]
        off = pl.multiple_of(s * bs, bs)
        xcols = x_ref[:, pl.ds(off, bs)].astype(jnp.float32)
        drift_ref[:, pl.ds(off, bs)] = rows[:ncomp] / rows[ncomp : ncomp + 1] - xcols
        return carry

    lax.fori_loop(0, nblk, block, 0)


def _specs(kinds):
    return [pl.BlockSpec(memory_space=pltpu.SMEM if k == "s" else pltpu.VMEM) for k in kinds]


def local(source_coords, target_coords, target_potential, fetch_blocks, pair_slots, pair_counts):
    ncomp = source_coords.shape[0]
    nblk = pair_counts.shape[0]
    bs = source_coords.shape[1] // nblk
    peers = lax.axis_size("blocks")
    cap = fetch_blocks.shape[2]
    nslot = peers * cap
    most = pair_slots.shape[1]
    log_mass = -math.log(peers * nblk * bs)
    assert most % TAIL == 0

    wanted = fetch_blocks[0]
    me = lax.axis_index("blocks")
    fetch_all = lax.all_to_all(
        jnp.broadcast_to(wanted[None], (peers, peers, cap)), "blocks", split_axis=0, concat_axis=0, tiled=True
    )
    asked = lax.dynamic_index_in_dim(fetch_all, me, axis=1, keepdims=False)
    asked_local = (asked % nblk).reshape(-1)

    potential_here = target_potential.reshape(nblk, bs)
    high_wide = lax.reduce_precision(potential_here, exponent_bits=8, mantissa_bits=7)
    rest = potential_here - high_wide
    middle_wide = lax.reduce_precision(rest, exponent_bits=8, mantissa_bits=7)
    high = high_wide.astype(jnp.bfloat16)
    middle = middle_wide.astype(jnp.bfloat16)
    low = (rest - middle_wide).astype(jnp.bfloat16)
    target_blocks = jnp.concatenate(
        [jnp.transpose(target_coords.reshape(ncomp, nblk, bs), (1, 0, 2)), high[:, None], middle[:, None], low[:, None]],
        axis=1,
    )
    send = target_blocks[asked_local].reshape(peers, cap, ncomp + 3, bs)
    came = lax.all_to_all(send, "blocks", split_axis=0, concat_axis=0, tiled=True).reshape(nslot, ncomp + 3, bs)
    pieces = came[:, ncomp:, :].astype(jnp.float32)
    slot_potential = (pieces[:, 0:1] + pieces[:, 1:2]) + pieces[:, 2:3]
    came_coords = came[:, :ncomp, :]
    came_wide = came_coords.astype(jnp.float32)
    quarter_ny = 0.25 * jnp.sum(came_wide * came_wide, axis=1, keepdims=True)
    slot_coords = jnp.concatenate(
        [
            came_coords,
            jnp.ones((nslot, 1, bs), jnp.bfloat16),
            jnp.zeros((nslot, PADDED - ncomp - 1, bs), jnp.bfloat16),
        ],
        axis=1,
    )
    slot_rows = jnp.concatenate(
        [jnp.transpose(slot_coords, (0, 2, 1)), jnp.zeros((nslot, bs, bs - PADDED), jnp.bfloat16)], axis=2
    )
    halved = (source_coords.astype(jnp.float32) * 0.5).astype(jnp.bfloat16)
    halved = jnp.concatenate([halved, jnp.zeros((PADDED - ncomp, nblk * bs), jnp.bfloat16)], axis=0)
    source_rows = jnp.transpose(halved.reshape(PADDED, nblk, bs), (1, 2, 0))
    flat_slots = pair_slots.reshape(-1)

    vmem = 48 * 1024 * 1024
    scratch = [pltpu.VMEM((nslot, 1, bs), jnp.float32), pltpu.VMEM((most, bs, bs), jnp.float32)]
    gather_all = peers * nslot * bs * 4 <= (1 << 20)
    copies = peers if gather_all else 1
    sweep = pl.pallas_call(
        functools.partial(sweep_kernel, most=most, log_mass=log_mass),
        out_shape=jax.ShapeDtypeStruct((copies, nslot, 1, bs), jnp.float32),
        in_specs=_specs("ssvvvv"),
        out_specs=_specs("v")[0],
        scratch_shapes=[pltpu.VMEM((nslot, 1, bs), jnp.float32)] * 2 + scratch[1:],
        compiler_params=pltpu.CompilerParams(vmem_limit_bytes=vmem),
    )
    final = pl.pallas_call(
        functools.partial(final_kernel, most=most, log_mass=log_mass, ncomp=ncomp),
        out_shape=(
            jax.ShapeDtypeStruct((nblk, 1, bs), jnp.float32),
            jax.ShapeDtypeStruct((ncomp, nblk * bs), jnp.float32),
        ),
        in_specs=_specs("ssvvvvv"),
        out_specs=tuple(_specs("vv")),
        scratch_shapes=scratch[1:],
        compiler_params=pltpu.CompilerParams(vmem_limit_bytes=vmem),
    )

    def combine(values, match, previous, axes):
        merged = jnp.max(jnp.where(match, values, floor_value), axis=axes)
        summed = jnp.sum(jnp.where(match, jnp.exp(values - jnp.expand_dims(merged, axes)), 0.0), axis=axes)
        reached = merged > 0.5 * floor_value
        return jnp.where(reached, log_mass - (merged + jnp.log(jnp.where(reached, summed, 1.0))), previous)

    owned = (asked_local.reshape(peers, cap)[None] == jnp.arange(nblk, dtype=jnp.int32)[:, None, None])[..., None]
    if gather_all:
        fetched = jnp.transpose(fetch_all, (1, 0, 2))[:, None, :, :] == wanted[:, :, None, None]
        fetched = fetched[..., None]
    for sweep_index in range(SWEEPS):
        lse = sweep(
            flat_slots, pair_counts, source_rows, slot_coords, slot_potential - quarter_ny, slot_potential
        )
        if gather_all:
            came = lax.all_to_all(lse, "blocks", split_axis=0, concat_axis=0, tiled=True).reshape(peers, peers, cap, bs)
            mine = lax.dynamic_index_in_dim(came, me, axis=1, keepdims=False)
            potential_here = combine(mine[None], owned, potential_here, (1, 2))
            by_owner = jnp.transpose(came, (1, 0, 2, 3))[:, None]
            slot_potential = combine(
                by_owner, fetched, slot_potential.reshape(peers, cap, bs), (2, 3)
            ).reshape(nslot, 1, bs)
        else:
            came = lax.all_to_all(
                lse.reshape(peers, cap, bs), "blocks", split_axis=0, concat_axis=0, tiled=True
            )
            potential_here = combine(came[None], owned, potential_here, (1, 2))
            send_potential = potential_here[asked_local].reshape(peers, cap, bs)
            slot_potential = lax.all_to_all(
                send_potential, "blocks", split_axis=0, concat_axis=0, tiled=True
            ).reshape(nslot, 1, bs)

    source_side, drift = final(
        flat_slots, pair_counts, source_rows, source_coords, slot_coords, slot_rows, slot_potential - quarter_ny
    )
    return (source_side.reshape(-1), potential_here.reshape(-1), drift)


def solution(mesh):
    return jax.shard_map(
        local,
        mesh=mesh,
        in_specs=(
            P(None, ("groups", "blocks")),
            P(None, ("groups", "blocks")),
            P(("groups", "blocks")),
            P(("groups", "blocks"), None, None),
            P(("groups", "blocks"), None),
            P(("groups", "blocks")),
        ),
        out_specs=(P(("groups", "blocks")), P(("groups", "blocks")), P(None, ("groups", "blocks"))),
        check_vma=False,
    )
```
